256 devices in a mesh: ctx: 32 (over z, y), dp: 8 (over x, core).
Axes of the slice: x: 4, y: 4, z: 8, core: 2. Of those that a mesh axis runs over, the one named last changes fastest.
Arguments:
- query: bfloat16 [65536, 128], P(('dp', 'ctx')), parts along dimension 0, may hold values from -6 to 6
- key: bfloat16 [65536, 128], P(('dp', 'ctx')), parts along dimension 0, may hold values from -6 to 6
- value_in: bfloat16 [65536, 1024], P(('dp', 'ctx')), parts along dimension 0, may hold values from -6 to 6
- gate: bfloat16 [65536, 1024], P(('dp', 'ctx')), parts along dimension 0, may hold values from -6 to 6
- conv_weight: bfloat16 [3, 1024], replicated, may hold values from -3 to 3
- doc_lengths: int32 [256], P('dp'), parts along dimension 0, may hold values from 1 to 4096, 8192 in all
- d_out: bfloat16 [65536, 1024], P(('dp', 'ctx')), parts along dimension 0, may hold values from -6 to 6
Outputs:
- mixed: bfloat16 [65536, 1024], P(('dp', 'ctx')), parts along dimension 0
- grad_query: bfloat16 [65536, 128], P(('dp', 'ctx')), parts along dimension 0
- grad_key: bfloat16 [65536, 128], P(('dp', 'ctx')), parts along dimension 0
- grad_value: bfloat16 [65536, 1024], P(('dp', 'ctx')), parts along dimension 0
- grad_gate: bfloat16 [65536, 1024], P(('dp', 'ctx')), parts along dimension 0
The draws below stay inside these ranges and needn't reach their ends.
There are 8 independent parts, one for each index of `dp`. The reference program is written for one: setup_inputs(seed, part) draws one part's arguments, and reference() takes and returns one part's arrays. A program takes and returns all parts, laid end to end along the dimension named above; an argument that names none is the same for every part. Nothing has to cross between parts.
Inputs may be any that keep to these rules, and one draw needn't show every extreme that they name: `doc_lengths`: the 32 lengths sum to 8192; the longest is exactly 4096.
All inputs are finite; a program needn't handle non-finite values.
Results may differ from the reference program's by a relative error of at most 0.005.
Values may be sent and summed in bfloat16 or wider, within the bound.
No kernel may reach another device: no remote copies, remote signals or barrier semaphores. Data moves between devices by JAX's collectives and lax.ppermute only.
A program may use at most 128 MiB of HBM per device.

```python
import math
import jax
import jax.numpy as jnp
import numpy as np
from jax import lax

HEADS = 8
KD = 16
VD = 128
CONV = 3
TOK_DEV = 256
FEAT = 273
TOKENS = 8192
DOCS = 32
MOST_DOC = 4096
N_CTX = 32


def shard_levels(own_key, dims, pieces, low, largest):
    factor_of, own = 1.0, jax.random.fold_in(own_key, 6)
    for position, parts in pieces:
        steps = jnp.exp(jax.random.uniform(jax.random.fold_in(own, position), (parts,), jnp.float32, low / len(pieces), largest / len(pieces)))
        factor_of = factor_of * jnp.repeat(steps, dims[position] // parts).reshape([-1 if axis == position else 1 for axis in range(len(dims))])
    return factor_of


def profile(amount, total, reach, skew):
    loads = [(1 << 20) // math.isqrt(rank ** skew) + 1 for rank in range(2, amount + 1)]
    rest, given = total - reach - (amount - 1), [1] * (amount - 1)
    while rest > 0:
        free = [i for i in range(amount - 1) if given[i] < reach]
        mass, left = sum([loads[i] for i in free]), rest
        for i in free:
            more = min(reach - given[i], max(1, left * loads[i] // mass), rest)
            given[i] = given[i] + more
            rest = rest - more
    return np.array([reach] + given)


def ragged(key, amount, total, most, lean):
    if amount == 2:
        one = jax.random.randint(key, (), max(1, total - most), min(most, total - 1) + 1)
        return jnp.stack([one, total - one])
    tallies = jnp.asarray(profile(amount, total, most, lean), jnp.int32)
    twos = (amount - 1) // 2
    donor, sink = tallies[1:1 + 2 * twos:2], tallies[2:2 + 2 * twos:2]
    room = jnp.minimum(donor - 1, most - sink)
    moved = jax.random.randint(jax.random.fold_in(key, 1), (twos,), 0, 1 << 20) % (room + 1)
    tallies = tallies.at[1:1 + 2 * twos:2].set(donor - moved).at[2:2 + 2 * twos:2].set(sink + moved)
    return tallies[jax.random.permutation(jax.random.fold_in(key, 2), amount)]


def centred(key, extent, scale, limit, split=(), held_as=jnp.bfloat16):
    gain = shard_levels(key, extent, split, -0.22, 0.18) if split else 1.0
    array = jax.random.normal(key, extent, jnp.float32) * scale * gain
    return jnp.minimum(jnp.maximum(array, -limit), limit).astype(held_as)


def setup_inputs(seed: int = 0, part: int = 0) -> dict:
    streams_of = jax.random.split(jax.random.key(seed), 8)
    part_keys = jax.random.split(jax.random.fold_in(streams_of[7], part), 8)
    query = centred(part_keys[0], (TOKENS, HEADS * KD), 1.5, 6.0, ((0, 32),))
    key = centred(part_keys[1], (TOKENS, HEADS * KD), 1.5, 6.0, ((0, 32),))
    value_in = centred(part_keys[2], (TOKENS, HEADS * VD), 1.0, 6.0, ((0, 32),))
    gate = centred(part_keys[3], (TOKENS, HEADS * VD), 1.5, 6.0, ((0, 32),))
    conv_weight = centred(streams_of[4], (CONV, HEADS * VD), 0.6, 3.0)
    doc_lengths = ragged(part_keys[5], DOCS, TOKENS, MOST_DOC, 2).astype(jnp.int32)
    d_out = centred(part_keys[6], (TOKENS, HEADS * VD), 1.0, 6.0, ((0, 32),))
    return dict(query=query, key=key, value_in=value_in, gate=gate, conv_weight=conv_weight, doc_lengths=doc_lengths, d_out=d_out)


highest = lax.Precision.HIGHEST
quad_scale = 1.0 / (4.0 * math.sqrt(2.0))

def document_ids(lengths, positions):
    ends = jnp.cumsum(lengths, dtype=jnp.int32)
    counted = lax.optimization_barrier(jnp.sum((ends[None, :] <= positions[:, None]).astype(jnp.int32), axis=1)).astype(jnp.int32)
    return jnp.where(positions < 0, jnp.int32(-1), counted).astype(jnp.int32)

def features(inputs):
    ones_col = jnp.ones(inputs.shape[:2] + (1,), jnp.float32)
    outer = (inputs[..., :, None] * inputs[..., None, :]).reshape(inputs.shape[0], inputs.shape[1], -1)
    return jnp.concatenate([ones_col, 0.5 * inputs, quad_scale * outer], axis=-1)

def block_step(carry, block):
    state, norm_state, prev_doc = carry
    q_block, k_block, v_block, d_block = block
    scores = jnp.einsum('thd,shd->hts', q_block, k_block, precision=highest) * 0.25
    kernel = 1.0 + scores + 0.5 * scores * scores
    places = jnp.arange(q_block.shape[0], dtype=jnp.int32)
    allowed = (places[:, None] >= places[None, :]) & (d_block[:, None] == d_block[None, :])
    weights = jnp.where(allowed[None], kernel, 0.0)
    numerator = jnp.einsum('hts,shv->thv', weights, v_block, precision=highest)
    denominator = jnp.transpose(lax.optimization_barrier(jnp.sum(weights, axis=2)), (1, 0))
    phi_query = features(q_block)
    phi_key = features(k_block)
    inside = (d_block == prev_doc).astype(jnp.float32)
    numerator = numerator + inside[:, None, None] * jnp.einsum('thf,hfv->thv', phi_query, state, precision=highest)
    denominator = denominator + inside[:, None] * jnp.einsum('thf,hf->th', phi_query, norm_state, precision=highest)
    attended = numerator / denominator[:, :, None]
    last_doc = d_block[-1]
    last_mask = (d_block == last_doc).astype(jnp.float32)
    restart = (last_doc != prev_doc).astype(jnp.float32)
    masked_key = phi_key * last_mask[:, None, None]
    local_state = jnp.einsum('thf,thv->hfv', masked_key, v_block, precision=highest)
    local_norm = lax.optimization_barrier(jnp.sum(masked_key, axis=0))
    new_state = local_state + (1.0 - restart) * state
    new_norm = local_norm + (1.0 - restart) * norm_state
    return ((new_state, new_norm, last_doc), attended)

def core(q_float, k_float, v_float, doc_ids):
    q_blocks = q_float.reshape(N_CTX, TOK_DEV, HEADS, KD)
    k_blocks = k_float.reshape(N_CTX, TOK_DEV, HEADS, KD)
    v_blocks = v_float.reshape(N_CTX, TOK_DEV, HEADS, VD)
    d_blocks = doc_ids.reshape(N_CTX, TOK_DEV)
    start = (jnp.zeros((HEADS, FEAT, VD), jnp.float32), jnp.zeros((HEADS, FEAT), jnp.float32), jnp.int32(-1))
    final, outputs = lax.scan(jax.checkpoint(block_step), start, (q_blocks, k_blocks, v_blocks, d_blocks))
    return outputs.reshape(TOKENS, HEADS * VD)

def reference(query, key, value_in, gate, conv_weight, doc_lengths, d_out):
    positions = jnp.arange(TOKENS, dtype=jnp.int32)
    doc_ids = document_ids(doc_lengths, positions)
    channels = HEADS * VD
    inputs = value_in.astype(jnp.float32)
    taps = conv_weight.astype(jnp.float32)
    convolved = jnp.zeros((TOKENS, channels), jnp.float32)
    for offset in range(CONV):
        shifted = jnp.concatenate([jnp.zeros((offset, channels), jnp.float32), inputs[:TOKENS - offset]], axis=0)
        shifted_ids = jnp.concatenate([jnp.full((offset,), -2, jnp.int32), doc_ids[:TOKENS - offset]], axis=0)
        keep = (shifted_ids == doc_ids).astype(jnp.float32)
        convolved = convolved + taps[offset][None, :] * shifted * keep[:, None]
    opening = jax.nn.sigmoid(gate.astype(jnp.float32))
    value = (convolved * opening).astype(jnp.bfloat16)
    q_float = query.astype(jnp.float32).reshape(TOKENS, HEADS, KD)
    k_float = key.astype(jnp.float32).reshape(TOKENS, HEADS, KD)
    v_float = value.astype(jnp.float32).reshape(TOKENS, HEADS, VD)
    attended, pullback = jax.vjp(lambda aa, bb, cc: core(aa, bb, cc, doc_ids), q_float, k_float, v_float)
    grad_q, grad_k, grad_core = pullback(d_out.astype(jnp.float32))
    grad_core = grad_core.reshape(TOKENS, channels)
    grad_gate = grad_core * convolved * opening * (1.0 - opening)
    grad_conv = grad_core * opening
    grad_value = jnp.zeros((TOKENS, channels), jnp.float32)
    for offset in range(CONV):
        ahead = jnp.concatenate([grad_conv[offset:], jnp.zeros((offset, channels), jnp.float32)], axis=0)
        ahead_ids = jnp.concatenate([doc_ids[offset:], jnp.full((offset,), DOCS + 1, jnp.int32)], axis=0)
        keep = (ahead_ids == doc_ids).astype(jnp.float32)
        grad_value = grad_value + taps[offset][None, :] * ahead * keep[:, None]
    return (attended.astype(jnp.bfloat16), grad_q.reshape(TOKENS, HEADS * KD).astype(jnp.bfloat16), grad_k.reshape(TOKENS, HEADS * KD).astype(jnp.bfloat16), grad_value.astype(jnp.bfloat16), grad_gate.astype(jnp.bfloat16))
```

```python
import math

import jax
import jax.numpy as jnp
from jax import lax
from jax.sharding import PartitionSpec as P

HEADS = 8
KD = 16
VD = 128
CONV = 3


highest = lax.Precision.HIGHEST
quad_scale = 1.0 / (4.0 * math.sqrt(2.0))


def shifted(block, axis, distance):
    devices = range(lax.axis_size(axis))
    route = [(i - distance, i) for i in devices if i - distance in devices]
    return lax.ppermute(block, axis, route)


def document_ids(lengths, positions):
    ends = jnp.cumsum(lengths, dtype=jnp.int32)
    counted = jnp.sum((ends[None, :] <= positions[:, None]).astype(jnp.int32), axis=1)
    return jnp.where(positions < 0, jnp.int32(-1), counted)


def feature_rows(values):
    spread = jnp.transpose(values, (1, 2, 0))
    head_count, width, token_count = spread.shape
    ones_row = jnp.ones((head_count, 1, token_count), jnp.float32)
    outer = (spread[:, :, None, :] * spread[:, None, :, :]).reshape(
        head_count, width * width, token_count
    )
    return (jnp.concatenate([ones_row, 0.5 * spread, quad_scale * outer], axis=1), spread)


def feature_grad(grad_phi, spread):
    width = spread.shape[1]
    linear = 0.5 * grad_phi[:, 1 : 1 + width]
    quad = grad_phi[:, 1 + width :].reshape(spread.shape[0], width, width, spread.shape[2])
    paired = quad + jnp.transpose(quad, (0, 2, 1, 3))
    return linear + quad_scale * jnp.einsum("hijt,hjt->hit", paired, spread, precision=highest)


def block_flags(doc_lengths, devices, rows):
    firsts = jnp.arange(devices, dtype=jnp.int32) * rows
    prev_docs = document_ids(doc_lengths, firsts - 1)
    first_docs = document_ids(doc_lengths, firsts)
    last_docs = document_ids(doc_lengths, firsts + rows - 1)
    next_docs = document_ids(doc_lengths, firsts + rows)
    return (last_docs != prev_docs).astype(jnp.int32), (first_docs != next_docs).astype(jnp.int32)


def scan_masks(restart, closes):
    devices = restart.shape[0]
    order = jnp.arange(devices, dtype=jnp.int32)
    target = order[:, None]
    source = order[None, :]
    restarts_upto = jnp.cumsum(restart)
    closes_upto = jnp.cumsum(closes)
    gap_fwd = restarts_upto[jnp.maximum(target - 1, 0)] - restarts_upto[source]
    forward = (source < target) & (gap_fwd == 0)
    gap_bwd = closes_upto[jnp.maximum(source - 1, 0)] - closes_upto[target]
    backward = (source > target) & (gap_bwd == 0)
    return forward.astype(jnp.float32), backward.astype(jnp.float32)


def state_scan(local_state, local_norm, mask):
    devices = mask.shape[0]
    heads, feats, width = local_state.shape
    state_rows = heads * feats
    norm_rows = -(-(heads * feats) // width)
    total_rows = -(-(state_rows + norm_rows) // devices) * devices
    flat_norm = jnp.pad(local_norm.reshape(-1), (0, norm_rows * width - heads * feats))
    packed = jnp.concatenate(
        [
            local_state.reshape(state_rows, width),
            flat_norm.reshape(norm_rows, width),
            jnp.zeros((total_rows - state_rows - norm_rows, width), jnp.float32),
        ],
        axis=0,
    ).reshape(devices, total_rows // devices, width)
    chunks = lax.all_to_all(packed, "ctx", 0, 0, tiled=True)
    summed = jnp.einsum("ij,jrc->irc", mask, chunks, precision=highest)
    back = lax.all_to_all(summed, "ctx", 0, 0, tiled=True).reshape(total_rows, width)
    state_in = back[:state_rows].reshape(heads, feats, width)
    norm_in = back[state_rows : state_rows + norm_rows].reshape(-1)[: heads * feats]
    return (state_in, norm_in.reshape(heads, feats))


def local(query, key, value_in, gate, conv_weight, doc_lengths, d_out):
    tok_rows = query.shape[0]
    channels = value_in.shape[1]
    dev_index = lax.axis_index("ctx")
    first_pos = dev_index * tok_rows
    local_pos = jnp.arange(tok_rows, dtype=jnp.int32)
    doc_ids = document_ids(doc_lengths, first_pos + local_pos)
    edge_docs = document_ids(doc_lengths, first_pos + jnp.array([-1, tok_rows], jnp.int32))
    prev_doc = edge_docs[0]
    next_doc = edge_docs[1]
    before_ids = document_ids(
        doc_lengths, first_pos - (CONV - 1) + jnp.arange(CONV - 1, dtype=jnp.int32)
    )
    after_ids = document_ids(
        doc_lengths, first_pos + tok_rows + jnp.arange(CONV - 1, dtype=jnp.int32)
    )
    taps = conv_weight.astype(jnp.float32)
    earlier = shifted(value_in[tok_rows - (CONV - 1) :], "ctx", 1)
    extended = jnp.concatenate([earlier, value_in], axis=0)
    extended_ids = jnp.concatenate([before_ids, doc_ids], axis=0)
    convolved = jnp.zeros((tok_rows, channels), jnp.float32)
    for offset in range(CONV):
        lower_row = CONV - 1 - offset
        keep = (extended_ids[lower_row : lower_row + tok_rows] == doc_ids).astype(jnp.float32)
        convolved = (
            convolved
            + taps[offset][None, :]
            * extended[lower_row : lower_row + tok_rows].astype(jnp.float32)
            * keep[:, None]
        )
    opening = jax.nn.sigmoid(gate.astype(jnp.float32))
    value_rows = (convolved * opening).astype(jnp.bfloat16)
    q_float = query.astype(jnp.float32).reshape(tok_rows, HEADS, KD)
    k_float = key.astype(jnp.float32).reshape(tok_rows, HEADS, KD)
    v_float = value_rows.astype(jnp.float32).reshape(tok_rows, HEADS, VD)
    scores = jnp.einsum("thd,shd->hts", q_float, k_float, precision=highest) * 0.25
    kernel = 1.0 + scores + 0.5 * scores * scores
    allowed = (local_pos[:, None] >= local_pos[None, :]) & (doc_ids[:, None] == doc_ids[None, :])
    weights = jnp.where(allowed[None], kernel, 0.0)
    numerator = jnp.einsum("hts,shv->thv", weights, v_float, precision=highest)
    denominator = jnp.transpose(jnp.sum(weights, axis=2), (1, 0))
    phi_query, spread_query = feature_rows(q_float)
    phi_key, spread_key = feature_rows(k_float)
    last_mask = (doc_ids == doc_ids[tok_rows - 1]).astype(jnp.float32)
    masked_key = phi_key * last_mask[None, None, :]
    local_state = jnp.einsum("hft,thv->hfv", masked_key, v_float, precision=highest)
    local_norm = jnp.sum(masked_key, axis=2)
    restart_all, closes_all = block_flags(doc_lengths, lax.axis_size("ctx"), tok_rows)
    forward_mask, backward_mask = scan_masks(restart_all, closes_all)
    state_in, norm_in = state_scan(local_state, local_norm, forward_mask)
    inside = (doc_ids == prev_doc).astype(jnp.float32)
    numerator = numerator + inside[:, None, None] * jnp.einsum(
        "hft,hfv->thv", phi_query, state_in, precision=highest
    )
    denominator = denominator + inside[:, None] * jnp.einsum(
        "hft,hf->th", phi_query, norm_in, precision=highest
    )
    attended = numerator / denominator[:, :, None]
    mixed = attended.reshape(tok_rows, HEADS * VD).astype(jnp.bfloat16)
    upstream = d_out.astype(jnp.float32).reshape(tok_rows, HEADS, VD)
    grad_num = upstream / denominator[:, :, None]
    grad_den = -jnp.sum(upstream * attended, axis=2) / denominator
    first_mask = (doc_ids == doc_ids[0]).astype(jnp.float32)
    masked_query = phi_query * first_mask[None, None, :]
    back_state = jnp.einsum("hft,thv->hfv", masked_query, grad_num, precision=highest)
    back_norm = jnp.einsum("hft,th->hf", masked_query, grad_den, precision=highest)
    grad_state_in, grad_norm_in = state_scan(back_state, back_norm, backward_mask)
    outside = (doc_ids == next_doc).astype(jnp.float32)
    grad_v = jnp.einsum("hts,thv->shv", weights, grad_num, precision=highest)
    grad_v = grad_v + outside[:, None, None] * jnp.einsum(
        "hfs,hfv->shv", phi_key, grad_state_in, precision=highest
    )
    grad_weights = (
        jnp.einsum("thv,shv->hts", grad_num, v_float, precision=highest)
        + jnp.transpose(grad_den, (1, 0))[:, :, None]
    )
    grad_scores = jnp.where(allowed[None], grad_weights * (1.0 + scores), 0.0)
    grad_q = jnp.einsum("hts,shd->thd", grad_scores, k_float, precision=highest) * 0.25
    grad_k = jnp.einsum("hts,thd->shd", grad_scores, q_float, precision=highest) * 0.25
    grad_phi_query = inside[None, None, :] * (
        jnp.einsum("hfv,thv->hft", state_in, grad_num, precision=highest)
        + norm_in[:, :, None] * jnp.transpose(grad_den, (1, 0))[:, None, :]
    )
    grad_phi_key = outside[None, None, :] * (
        jnp.einsum("hfv,shv->hfs", grad_state_in, v_float, precision=highest)
        + grad_norm_in[:, :, None]
    )
    grad_q = grad_q + jnp.transpose(feature_grad(grad_phi_query, spread_query), (2, 0, 1))
    grad_k = grad_k + jnp.transpose(feature_grad(grad_phi_key, spread_key), (2, 0, 1))
    grad_query = grad_q.reshape(tok_rows, HEADS * KD).astype(jnp.bfloat16)
    grad_key = grad_k.reshape(tok_rows, HEADS * KD).astype(jnp.bfloat16)
    grad_core = grad_v.reshape(tok_rows, channels)
    grad_gate = (grad_core * convolved * opening * (1.0 - opening)).astype(jnp.bfloat16)
    grad_conv = grad_core * opening
    later_rows = shifted(grad_conv[: CONV - 1], "ctx", -1)
    ahead = jnp.concatenate([grad_conv, later_rows], axis=0)
    ahead_ids = jnp.concatenate([doc_ids, after_ids], axis=0)
    grad_value = jnp.zeros((tok_rows, channels), jnp.float32)
    for offset in range(CONV):
        keep = (ahead_ids[offset : offset + tok_rows] == doc_ids).astype(jnp.float32)
        grad_value = (
            grad_value + taps[offset][None, :] * ahead[offset : offset + tok_rows] * keep[:, None]
        )
    return (mixed, grad_query, grad_key, grad_value.astype(jnp.bfloat16), grad_gate)


def solution(mesh):
    placed = (
        P(("dp", "ctx"), None),
        P(("dp", "ctx"), None),
        P(("dp", "ctx"), None),
        P(("dp", "ctx"), None),
        P(),
        P("dp"),
        P(("dp", "ctx"), None),
    )
    return jax.shard_map(
        local,
        mesh=mesh,
        in_specs=placed,
        out_specs=(
            P(("dp", "ctx"), None),
            P(("dp", "ctx"), None),
            P(("dp", "ctx"), None),
            P(("dp", "ctx"), None),
            P(("dp", "ctx"), None),
        ),
        check_vma=False,
    )
```

```python
import math

import jax
import numpy as np
import jax.numpy as jnp
from jax import lax
from jax.sharding import PartitionSpec as P

HEADS = 8
KD = 16
VD = 128
CONV = 3


highest = lax.Precision.HIGHEST
quad_scale = 1.0 / (4.0 * math.sqrt(2.0))


def shifted(block, axis, distance):
    devices = range(lax.axis_size(axis))
    route = [(i - distance, i) for i in devices if i - distance in devices]
    return lax.ppermute(block, axis, route)


def document_ids(lengths, positions):
    ends = jnp.cumsum(lengths, dtype=jnp.int32)
    counted = jnp.sum((ends[None, :] <= positions[:, None]).astype(jnp.int32), axis=1)
    return jnp.where(positions < 0, jnp.int32(-1), counted)


def pair_tables(width):
    rows, cols = np.triu_indices(width)
    weight = np.where(rows == cols, quad_scale, quad_scale * math.sqrt(2.0)).astype(np.float32)
    place = np.zeros((width, width), np.int32)
    place[rows, cols] = np.arange(rows.size)
    place[cols, rows] = np.arange(rows.size)
    spread_weight = np.where(np.eye(width, dtype=bool), 2.0, 1.0) * weight[place]
    return rows, cols, weight, place.reshape(-1), spread_weight.astype(np.float32).reshape(-1)


def feature_rows(values):
    spread = jnp.transpose(values, (1, 2, 0))
    head_count, width, token_count = spread.shape
    rows, cols, weight, _, _ = pair_tables(width)
    ones_row = jnp.ones((head_count, 1, token_count), jnp.float32)
    pieces = []
    for i in range(width):
        pieces.append(spread[:, i : i + 1, :] * spread[:, i:, :])
    outer = jnp.concatenate(pieces, axis=1) * jnp.asarray(weight)[None, :, None]
    return (jnp.concatenate([ones_row, 0.5 * spread, outer], axis=1), spread)


def feature_grad(grad_phi, spread):
    head_count, width, token_count = spread.shape
    _, _, _, place, spread_weight = pair_tables(width)
    linear = 0.5 * grad_phi[:, 1 : 1 + width]
    quad = grad_phi[:, 1 + width :]
    paired = jnp.take(quad, jnp.asarray(place), axis=1) * jnp.asarray(spread_weight)[None, :, None]
    paired = paired.reshape(head_count, width, width, token_count)
    return linear + jnp.einsum("hijt,hjt->hit", paired, spread, precision=highest)


def block_flags(doc_lengths, devices, rows):
    firsts = jnp.arange(devices, dtype=jnp.int32) * rows
    prev_docs = document_ids(doc_lengths, firsts - 1)
    first_docs = document_ids(doc_lengths, firsts)
    last_docs = document_ids(doc_lengths, firsts + rows - 1)
    next_docs = document_ids(doc_lengths, firsts + rows)
    return (last_docs != prev_docs).astype(jnp.int32), (first_docs != next_docs).astype(jnp.int32)


def scan_masks(restart, closes):
    devices = restart.shape[0]
    order = jnp.arange(devices, dtype=jnp.int32)
    target = order[:, None]
    source = order[None, :]
    restarts_upto = jnp.cumsum(restart)
    closes_upto = jnp.cumsum(closes)
    gap_fwd = restarts_upto[jnp.maximum(target - 1, 0)] - restarts_upto[source]
    forward = (source < target) & (gap_fwd == 0)
    gap_bwd = closes_upto[jnp.maximum(source - 1, 0)] - closes_upto[target]
    backward = (source > target) & (gap_bwd == 0)
    return forward.astype(jnp.float32), backward.astype(jnp.float32)


def state_scan(local_state, local_norm, mask):
    devices = mask.shape[0]
    heads, feats, width = local_state.shape
    state_rows = heads * feats
    norm_rows = -(-(heads * feats) // width)
    total_rows = -(-(state_rows + norm_rows) // devices) * devices
    flat_norm = jnp.pad(local_norm.reshape(-1), (0, norm_rows * width - heads * feats))
    packed = jnp.concatenate(
        [
            local_state.reshape(state_rows, width),
            flat_norm.reshape(norm_rows, width),
            jnp.zeros((total_rows - state_rows - norm_rows, width), jnp.float32),
        ],
        axis=0,
    ).reshape(devices, total_rows // devices, width)
    chunks = lax.all_to_all(packed, "ctx", 0, 0, tiled=True)
    summed = jnp.einsum("ij,jrc->irc", mask, chunks, precision=highest)
    back = lax.all_to_all(summed, "ctx", 0, 0, tiled=True).reshape(total_rows, width)
    state_in = back[:state_rows].reshape(heads, feats, width)
    norm_in = back[state_rows : state_rows + norm_rows].reshape(-1)[: heads * feats]
    return (state_in, norm_in.reshape(heads, feats))


def local(query, key, value_in, gate, conv_weight, doc_lengths, d_out):
    tok_rows = query.shape[0]
    channels = value_in.shape[1]
    dev_index = lax.axis_index("ctx")
    first_pos = dev_index * tok_rows
    local_pos = jnp.arange(tok_rows, dtype=jnp.int32)
    doc_ids = document_ids(doc_lengths, first_pos + local_pos)
    edge_docs = document_ids(doc_lengths, first_pos + jnp.array([-1, tok_rows], jnp.int32))
    prev_doc = edge_docs[0]
    next_doc = edge_docs[1]
    before_ids = document_ids(
        doc_lengths, first_pos - (CONV - 1) + jnp.arange(CONV - 1, dtype=jnp.int32)
    )
    after_ids = document_ids(
        doc_lengths, first_pos + tok_rows + jnp.arange(CONV - 1, dtype=jnp.int32)
    )
    taps = conv_weight.astype(jnp.float32)
    earlier = shifted(value_in[tok_rows - (CONV - 1) :], "ctx", 1)
    extended = jnp.concatenate([earlier, value_in], axis=0)
    extended_ids = jnp.concatenate([before_ids, doc_ids], axis=0)
    convolved = jnp.zeros((tok_rows, channels), jnp.float32)
    for offset in range(CONV):
        lower_row = CONV - 1 - offset
        keep = (extended_ids[lower_row : lower_row + tok_rows] == doc_ids).astype(jnp.float32)
        convolved = (
            convolved
            + taps[offset][None, :]
            * extended[lower_row : lower_row + tok_rows].astype(jnp.float32)
            * keep[:, None]
        )
    opening = jax.nn.sigmoid(gate.astype(jnp.float32))
    value_rows = (convolved * opening).astype(jnp.bfloat16)
    q_float = query.astype(jnp.float32).reshape(tok_rows, HEADS, KD)
    k_float = key.astype(jnp.float32).reshape(tok_rows, HEADS, KD)
    v_float = value_rows.astype(jnp.float32).reshape(tok_rows, HEADS, VD)
    scores = jnp.einsum("thd,shd->hts", q_float, k_float, precision=highest) * 0.25
    kernel = 1.0 + scores + 0.5 * scores * scores
    allowed = (local_pos[:, None] >= local_pos[None, :]) & (doc_ids[:, None] == doc_ids[None, :])
    weights = jnp.where(allowed[None], kernel, 0.0)
    numerator = jnp.einsum("hts,shv->thv", weights, v_float, precision=highest)
    denominator = jnp.transpose(jnp.sum(weights, axis=2), (1, 0))
    phi_query, spread_query = feature_rows(q_float)
    phi_key, spread_key = feature_rows(k_float)
    last_mask = (doc_ids == doc_ids[tok_rows - 1]).astype(jnp.float32)
    masked_key = phi_key * last_mask[None, None, :]
    local_state = jnp.einsum("hft,thv->hfv", masked_key, v_float, precision=highest)
    local_norm = jnp.sum(masked_key, axis=2)
    restart_all, closes_all = block_flags(doc_lengths, lax.axis_size("ctx"), tok_rows)
    forward_mask, backward_mask = scan_masks(restart_all, closes_all)
    state_in, norm_in = state_scan(local_state, local_norm, forward_mask)
    inside = (doc_ids == prev_doc).astype(jnp.float32)
    numerator = numerator + inside[:, None, None] * jnp.einsum(
        "hft,hfv->thv", phi_query, state_in, precision=highest
    )
    denominator = denominator + inside[:, None] * jnp.einsum(
        "hft,hf->th", phi_query, norm_in, precision=highest
    )
    attended = numerator / denominator[:, :, None]
    mixed = attended.reshape(tok_rows, HEADS * VD).astype(jnp.bfloat16)
    upstream = d_out.astype(jnp.float32).reshape(tok_rows, HEADS, VD)
    grad_num = upstream / denominator[:, :, None]
    grad_den = -jnp.sum(upstream * attended, axis=2) / denominator
    first_mask = (doc_ids == doc_ids[0]).astype(jnp.float32)
    masked_query = phi_query * first_mask[None, None, :]
    back_state = jnp.einsum("hft,thv->hfv", masked_query, grad_num, precision=highest)
    back_norm = jnp.einsum("hft,th->hf", masked_query, grad_den, precision=highest)
    grad_state_in, grad_norm_in = state_scan(back_state, back_norm, backward_mask)
    outside = (doc_ids == next_doc).astype(jnp.float32)
    grad_v = jnp.einsum("hts,thv->shv", weights, grad_num, precision=highest)
    grad_v = grad_v + outside[:, None, None] * jnp.einsum(
        "hfs,hfv->shv", phi_key, grad_state_in, precision=highest
    )
    grad_weights = (
        jnp.einsum("thv,shv->hts", grad_num, v_float, precision=highest)
        + jnp.transpose(grad_den, (1, 0))[:, :, None]
    )
    grad_scores = jnp.where(allowed[None], grad_weights * (1.0 + scores), 0.0)
    grad_q = jnp.einsum("hts,shd->thd", grad_scores, k_float, precision=highest) * 0.25
    grad_k = jnp.einsum("hts,thd->shd", grad_scores, q_float, precision=highest) * 0.25
    grad_phi_query = inside[None, None, :] * (
        jnp.einsum("hfv,thv->hft", state_in, grad_num, precision=highest)
        + norm_in[:, :, None] * jnp.transpose(grad_den, (1, 0))[:, None, :]
    )
    grad_phi_key = outside[None, None, :] * (
        jnp.einsum("hfv,shv->hfs", grad_state_in, v_float, precision=highest)
        + grad_norm_in[:, :, None]
    )
    grad_q = grad_q + jnp.transpose(feature_grad(grad_phi_query, spread_query), (2, 0, 1))
    grad_k = grad_k + jnp.transpose(feature_grad(grad_phi_key, spread_key), (2, 0, 1))
    grad_query = grad_q.reshape(tok_rows, HEADS * KD).astype(jnp.bfloat16)
    grad_key = grad_k.reshape(tok_rows, HEADS * KD).astype(jnp.bfloat16)
    grad_core = grad_v.reshape(tok_rows, channels)
    grad_gate = (grad_core * convolved * opening * (1.0 - opening)).astype(jnp.bfloat16)
    grad_conv = grad_core * opening
    later_rows = shifted(grad_conv[: CONV - 1], "ctx", -1)
    ahead = jnp.concatenate([grad_conv, later_rows], axis=0)
    ahead_ids = jnp.concatenate([doc_ids, after_ids], axis=0)
    grad_value = jnp.zeros((tok_rows, channels), jnp.float32)
    for offset in range(CONV):
        keep = (ahead_ids[offset : offset + tok_rows] == doc_ids).astype(jnp.float32)
        grad_value = (
            grad_value + taps[offset][None, :] * ahead[offset : offset + tok_rows] * keep[:, None]
        )
    return (mixed, grad_query, grad_key, grad_value.astype(jnp.bfloat16), grad_gate)


def solution(mesh):
    placed = (
        P(("dp", "ctx"), None),
        P(("dp", "ctx"), None),
        P(("dp", "ctx"), None),
        P(("dp", "ctx"), None),
        P(),
        P("dp"),
        P(("dp", "ctx"), None),
    )
    return jax.shard_map(
        local,
        mesh=mesh,
        in_specs=placed,
        out_specs=(
            P(("dp", "ctx"), None),
            P(("dp", "ctx"), None),
            P(("dp", "ctx"), None),
            P(("dp", "ctx"), None),
            P(("dp", "ctx"), None),
        ),
        check_vma=False,
    )
```

```python
import math

import jax
import numpy as np
import jax.numpy as jnp
from jax import lax
from jax.sharding import PartitionSpec as P

HEADS = 8
KD = 16
VD = 128
CONV = 3


highest = lax.Precision.HIGHEST
high = lax.Precision.HIGH
quad_scale = 1.0 / (4.0 * math.sqrt(2.0))


def shifted(block, axis, distance):
    devices = range(lax.axis_size(axis))
    route = [(i - distance, i) for i in devices if i - distance in devices]
    return lax.ppermute(block, axis, route)


def document_ids(lengths, positions):
    ends = jnp.cumsum(lengths, dtype=jnp.int32)
    counted = jnp.sum((ends[None, :] <= positions[:, None]).astype(jnp.int32), axis=1)
    return jnp.where(positions < 0, jnp.int32(-1), counted)


def pair_tables(width):
    rows, cols = np.triu_indices(width)
    weight = np.where(rows == cols, quad_scale, quad_scale * math.sqrt(2.0)).astype(np.float32)
    place = np.zeros((width, width), np.int32)
    place[rows, cols] = np.arange(rows.size)
    place[cols, rows] = np.arange(rows.size)
    spread_weight = np.where(np.eye(width, dtype=bool), 2.0, 1.0) * weight[place]
    return rows, cols, weight, place.reshape(-1), spread_weight.astype(np.float32).reshape(-1)


def feature_rows(values):
    spread = jnp.transpose(values, (1, 2, 0))
    head_count, width, token_count = spread.shape
    rows, cols, weight, _, _ = pair_tables(width)
    ones_row = jnp.ones((head_count, 1, token_count), jnp.float32)
    pieces = []
    for i in range(width):
        pieces.append(spread[:, i : i + 1, :] * spread[:, i:, :])
    outer = jnp.concatenate(pieces, axis=1) * jnp.asarray(weight)[None, :, None]
    return (jnp.concatenate([ones_row, 0.5 * spread, outer], axis=1), spread)


def feature_grad(grad_phi, spread):
    head_count, width, token_count = spread.shape
    _, _, _, place, spread_weight = pair_tables(width)
    linear = 0.5 * grad_phi[:, 1 : 1 + width]
    quad = grad_phi[:, 1 + width :]
    paired = jnp.take(quad, jnp.asarray(place), axis=1) * jnp.asarray(spread_weight)[None, :, None]
    paired = paired.reshape(head_count, width, width, token_count)
    return linear + jnp.einsum("hijt,hjt->hit", paired, spread, precision=high)


def block_flags(doc_lengths, devices, rows):
    firsts = jnp.arange(devices, dtype=jnp.int32) * rows
    prev_docs = document_ids(doc_lengths, firsts - 1)
    first_docs = document_ids(doc_lengths, firsts)
    last_docs = document_ids(doc_lengths, firsts + rows - 1)
    next_docs = document_ids(doc_lengths, firsts + rows)
    return (last_docs != prev_docs).astype(jnp.int32), (first_docs != next_docs).astype(jnp.int32)


def scan_masks(restart, closes):
    devices = restart.shape[0]
    order = jnp.arange(devices, dtype=jnp.int32)
    target = order[:, None]
    source = order[None, :]
    restarts_upto = jnp.cumsum(restart)
    closes_upto = jnp.cumsum(closes)
    gap_fwd = restarts_upto[jnp.maximum(target - 1, 0)] - restarts_upto[source]
    forward = (source < target) & (gap_fwd == 0)
    gap_bwd = closes_upto[jnp.maximum(source - 1, 0)] - closes_upto[target]
    backward = (source > target) & (gap_bwd == 0)
    return forward.astype(jnp.float32), backward.astype(jnp.float32)


def state_scan(local_state, local_norm, mask):
    devices = mask.shape[0]
    heads, feats, width = local_state.shape
    norm_rows = -(-feats // width)
    head_rows = feats + norm_rows
    spare = (-heads * head_rows) % devices
    flat_norm = jnp.pad(local_norm, ((0, 0), (0, norm_rows * width - feats)))
    packed = jnp.concatenate(
        [local_state, flat_norm.reshape(heads, norm_rows, width)], axis=1
    ).reshape(heads * head_rows, width)
    if spare:
        packed = jnp.pad(packed, ((0, spare), (0, 0)))
    packed = packed.reshape(devices, -1, width)
    chunks = lax.all_to_all(packed, "ctx", 0, 0, tiled=True)
    summed = jnp.einsum("ij,jrc->irc", mask, chunks, precision=high)
    back = lax.all_to_all(summed, "ctx", 0, 0, tiled=True).reshape(-1, width)
    back = back[: heads * head_rows].reshape(heads, head_rows, width)
    state_in = back[:, :feats]
    norm_in = back[:, feats:].reshape(heads, norm_rows * width)[:, :feats]
    return (state_in, norm_in)


def local(query, key, value_in, gate, conv_weight, doc_lengths, d_out):
    tok_rows = query.shape[0]
    channels = value_in.shape[1]
    dev_index = lax.axis_index("ctx")
    first_pos = dev_index * tok_rows
    local_pos = jnp.arange(tok_rows, dtype=jnp.int32)
    doc_ids = document_ids(doc_lengths, first_pos + local_pos)
    edge_docs = document_ids(doc_lengths, first_pos + jnp.array([-1, tok_rows], jnp.int32))
    prev_doc = edge_docs[0]
    next_doc = edge_docs[1]
    before_ids = document_ids(
        doc_lengths, first_pos - (CONV - 1) + jnp.arange(CONV - 1, dtype=jnp.int32)
    )
    after_ids = document_ids(
        doc_lengths, first_pos + tok_rows + jnp.arange(CONV - 1, dtype=jnp.int32)
    )
    taps = conv_weight.astype(jnp.float32)
    earlier = shifted(value_in[tok_rows - (CONV - 1) :], "ctx", 1)
    extended = jnp.concatenate([earlier, value_in], axis=0)
    extended_ids = jnp.concatenate([before_ids, doc_ids], axis=0)
    convolved = jnp.zeros((tok_rows, channels), jnp.float32)
    for offset in range(CONV):
        lower_row = CONV - 1 - offset
        keep = (extended_ids[lower_row : lower_row + tok_rows] == doc_ids).astype(jnp.float32)
        convolved = (
            convolved
            + taps[offset][None, :]
            * extended[lower_row : lower_row + tok_rows].astype(jnp.float32)
            * keep[:, None]
        )
    opening = jax.nn.sigmoid(gate.astype(jnp.float32))
    value_rows = (convolved * opening).astype(jnp.bfloat16)
    q_float = query.astype(jnp.float32).reshape(tok_rows, HEADS, KD)
    k_float = key.astype(jnp.float32).reshape(tok_rows, HEADS, KD)
    v_float = value_rows.astype(jnp.float32).reshape(tok_rows, HEADS, VD)
    scores = (
        jnp.einsum(
            "thd,shd->hts",
            query.reshape(tok_rows, HEADS, KD),
            key.reshape(tok_rows, HEADS, KD),
            preferred_element_type=jnp.float32,
        )
        * 0.25
    )
    kernel = 1.0 + scores + 0.5 * scores * scores
    allowed = (local_pos[:, None] >= local_pos[None, :]) & (doc_ids[:, None] == doc_ids[None, :])
    weights = jnp.where(allowed[None], kernel, 0.0)
    numerator = jnp.einsum("hts,shv->thv", weights, v_float, precision=high)
    denominator = jnp.transpose(jnp.sum(weights, axis=2), (1, 0))
    phi_query, spread_query = feature_rows(q_float)
    phi_key, spread_key = feature_rows(k_float)
    last_mask = (doc_ids == doc_ids[tok_rows - 1]).astype(jnp.float32)
    masked_key = phi_key * last_mask[None, None, :]
    local_state = jnp.einsum("hft,thv->hfv", masked_key, v_float, precision=high)
    local_norm = jnp.sum(masked_key, axis=2)
    restart_all, closes_all = block_flags(doc_lengths, lax.axis_size("ctx"), tok_rows)
    forward_mask, backward_mask = scan_masks(restart_all, closes_all)
    state_in, norm_in = state_scan(local_state, local_norm, forward_mask)
    inside = (doc_ids == prev_doc).astype(jnp.float32)
    numerator = numerator + inside[:, None, None] * jnp.einsum(
        "hft,hfv->thv", phi_query, state_in, precision=high
    )
    denominator = denominator + inside[:, None] * jnp.einsum(
        "hft,hf->th", phi_query, norm_in, precision=high
    )
    attended = numerator / denominator[:, :, None]
    mixed = attended.reshape(tok_rows, HEADS * VD).astype(jnp.bfloat16)
    upstream = d_out.astype(jnp.float32).reshape(tok_rows, HEADS, VD)
    grad_num = upstream / denominator[:, :, None]
    grad_den = -jnp.sum(upstream * attended, axis=2) / denominator
    first_mask = (doc_ids == doc_ids[0]).astype(jnp.float32)
    masked_query = phi_query * first_mask[None, None, :]
    back_state = jnp.einsum("hft,thv->hfv", masked_query, grad_num, precision=high)
    back_norm = jnp.einsum("hft,th->hf", masked_query, grad_den, precision=high)
    grad_state_in, grad_norm_in = state_scan(back_state, back_norm, backward_mask)
    outside = (doc_ids == next_doc).astype(jnp.float32)
    grad_v = jnp.einsum("hts,thv->shv", weights, grad_num, precision=high)
    grad_v = grad_v + outside[:, None, None] * jnp.einsum(
        "hfs,hfv->shv", phi_key, grad_state_in, precision=high
    )
    grad_weights = (
        jnp.einsum("thv,shv->hts", grad_num, v_float, precision=high)
        + jnp.transpose(grad_den, (1, 0))[:, :, None]
    )
    grad_scores = jnp.where(allowed[None], grad_weights * (1.0 + scores), 0.0)
    grad_q = jnp.einsum("hts,shd->thd", grad_scores, k_float, precision=high) * 0.25
    grad_k = jnp.einsum("hts,thd->shd", grad_scores, q_float, precision=high) * 0.25
    grad_phi_query = inside[None, None, :] * (
        jnp.einsum("hfv,thv->hft", state_in, grad_num, precision=high)
        + norm_in[:, :, None] * jnp.transpose(grad_den, (1, 0))[:, None, :]
    )
    grad_phi_key = outside[None, None, :] * (
        jnp.einsum("hfv,shv->hfs", grad_state_in, v_float, precision=high)
        + grad_norm_in[:, :, None]
    )
    grad_q = grad_q + jnp.transpose(feature_grad(grad_phi_query, spread_query), (2, 0, 1))
    grad_k = grad_k + jnp.transpose(feature_grad(grad_phi_key, spread_key), (2, 0, 1))
    grad_query = grad_q.reshape(tok_rows, HEADS * KD).astype(jnp.bfloat16)
    grad_key = grad_k.reshape(tok_rows, HEADS * KD).astype(jnp.bfloat16)
    grad_core = grad_v.reshape(tok_rows, channels)
    grad_gate = (grad_core * convolved * opening * (1.0 - opening)).astype(jnp.bfloat16)
    grad_conv = grad_core * opening
    later_rows = shifted(grad_conv[: CONV - 1], "ctx", -1)
    ahead = jnp.concatenate([grad_conv, later_rows], axis=0)
    ahead_ids = jnp.concatenate([doc_ids, after_ids], axis=0)
    grad_value = jnp.zeros((tok_rows, channels), jnp.float32)
    for offset in range(CONV):
        keep = (ahead_ids[offset : offset + tok_rows] == doc_ids).astype(jnp.float32)
        grad_value = (
            grad_value + taps[offset][None, :] * ahead[offset : offset + tok_rows] * keep[:, None]
        )
    return (mixed, grad_query, grad_key, grad_value.astype(jnp.bfloat16), grad_gate)


def solution(mesh):
    placed = (
        P(("dp", "ctx"), None),
        P(("dp", "ctx"), None),
        P(("dp", "ctx"), None),
        P(("dp", "ctx"), None),
        P(),
        P("dp"),
        P(("dp", "ctx"), None),
    )
    return jax.shard_map(
        local,
        mesh=mesh,
        in_specs=placed,
        out_specs=(
            P(("dp", "ctx"), None),
            P(("dp", "ctx"), None),
            P(("dp", "ctx"), None),
            P(("dp", "ctx"), None),
            P(("dp", "ctx"), None),
        ),
        check_vma=False,
    )
```

```python
import math

import jax
import numpy as np
import jax.numpy as jnp
from jax import lax
from jax.sharding import PartitionSpec as P

HEADS = 8
KD = 16
VD = 128
CONV = 3


highest = lax.Precision.HIGHEST
high = lax.Precision.HIGH
quad_scale = 1.0 / (4.0 * math.sqrt(2.0))


def shifted(block, axis, distance):
    devices = range(lax.axis_size(axis))
    route = [(i - distance, i) for i in devices if i - distance in devices]
    return lax.ppermute(block, axis, route)


def document_ids(lengths, positions):
    ends = jnp.cumsum(lengths, dtype=jnp.int32)
    counted = jnp.sum((ends[None, :] <= positions[:, None]).astype(jnp.int32), axis=1)
    return jnp.where(positions < 0, jnp.int32(-1), counted)


def pair_tables(width):
    rows, cols = np.triu_indices(width)
    quad_weight = np.where(rows == cols, quad_scale, quad_scale * math.sqrt(2.0))
    first = np.concatenate([[-1], np.full(width, -1), rows])
    second = np.concatenate([[-1], np.arange(width), cols])
    scale = np.concatenate([[1.0], np.full(width, 0.5), quad_weight]).astype(np.float32)
    dims = np.arange(width)
    pick_first = (first[:, None] == dims[None, :]).astype(np.float32)
    pick_second = (second[:, None] == dims[None, :]).astype(np.float32)
    return pick_first, (first < 0).astype(np.float32), pick_second, (second < 0).astype(np.float32), scale


def feature_rows(values):
    token_count, head_count, width = values.shape
    pick_first, one_first, pick_second, one_second, scale = pair_tables(width)
    picks = jnp.asarray(np.stack([pick_first, pick_second]), jnp.bfloat16)
    chosen = jnp.einsum("pfd,thd->phft", picks, values, preferred_element_type=jnp.float32)
    left = chosen[0] + jnp.asarray(one_first)[None, :, None]
    right = chosen[1] + jnp.asarray(one_second)[None, :, None]
    return (jnp.asarray(scale)[None, :, None] * left * right, (left, right))


def feature_grad(grad_phi, factors):
    left, right = factors
    width = 16
    pick_first, _, pick_second, _, scale = pair_tables(width)
    scaled = grad_phi * jnp.asarray(scale)[None, :, None]
    picks = jnp.asarray(np.concatenate([pick_first, pick_second], axis=0))
    both = jnp.concatenate([scaled * right, scaled * left], axis=1)
    return jnp.einsum("fd,hft->thd", picks, both, precision=high)


def block_flags(doc_lengths, devices, rows):
    firsts = jnp.arange(devices, dtype=jnp.int32) * rows
    prev_docs = document_ids(doc_lengths, firsts - 1)
    first_docs = document_ids(doc_lengths, firsts)
    last_docs = document_ids(doc_lengths, firsts + rows - 1)
    next_docs = document_ids(doc_lengths, firsts + rows)
    return (last_docs != prev_docs).astype(jnp.int32), (first_docs != next_docs).astype(jnp.int32)


def scan_masks(restart, closes):
    devices = restart.shape[0]
    order = jnp.arange(devices, dtype=jnp.int32)
    target = order[:, None]
    source = order[None, :]
    restarts_upto = jnp.cumsum(restart)
    closes_upto = jnp.cumsum(closes)
    gap_fwd = restarts_upto[jnp.maximum(target - 1, 0)] - restarts_upto[source]
    forward = (source < target) & (gap_fwd == 0)
    gap_bwd = closes_upto[jnp.maximum(source - 1, 0)] - closes_upto[target]
    backward = (source > target) & (gap_bwd == 0)
    return forward.astype(jnp.float32), backward.astype(jnp.float32)


def state_scan(local_state, local_norm, mask):
    devices = mask.shape[0]
    heads, feats, width = local_state.shape
    norm_rows = -(-feats // width)
    head_rows = feats + norm_rows
    spare = (-heads * head_rows) % devices
    flat_norm = jnp.pad(local_norm, ((0, 0), (0, norm_rows * width - feats)))
    packed = jnp.concatenate(
        [local_state, flat_norm.reshape(heads, norm_rows, width)], axis=1
    ).reshape(heads * head_rows, width)
    if spare:
        packed = jnp.pad(packed, ((0, spare), (0, 0)))
    packed = packed.reshape(devices, -1, width)
    chunks = lax.all_to_all(packed, "ctx", 0, 0, tiled=True)
    summed = jnp.einsum("ij,jrc->irc", mask, chunks, precision=high)
    back = lax.all_to_all(summed, "ctx", 0, 0, tiled=True).reshape(-1, width)
    back = back[: heads * head_rows].reshape(heads, head_rows, width)
    state_in = back[:, :feats]
    norm_in = back[:, feats:].reshape(heads, norm_rows * width)[:, :feats]
    return (state_in, norm_in)


def local(query, key, value_in, gate, conv_weight, doc_lengths, d_out):
    tok_rows = query.shape[0]
    channels = value_in.shape[1]
    dev_index = lax.axis_index("ctx")
    first_pos = dev_index * tok_rows
    local_pos = jnp.arange(tok_rows, dtype=jnp.int32)
    doc_ids = document_ids(doc_lengths, first_pos + local_pos)
    edge_docs = document_ids(doc_lengths, first_pos + jnp.array([-1, tok_rows], jnp.int32))
    prev_doc = edge_docs[0]
    next_doc = edge_docs[1]
    before_ids = document_ids(
        doc_lengths, first_pos - (CONV - 1) + jnp.arange(CONV - 1, dtype=jnp.int32)
    )
    after_ids = document_ids(
        doc_lengths, first_pos + tok_rows + jnp.arange(CONV - 1, dtype=jnp.int32)
    )
    taps = conv_weight.astype(jnp.float32)
    earlier = shifted(value_in[tok_rows - (CONV - 1) :], "ctx", 1)
    extended = jnp.concatenate([earlier, value_in], axis=0)
    extended_ids = jnp.concatenate([before_ids, doc_ids], axis=0)
    convolved = jnp.zeros((tok_rows, channels), jnp.float32)
    for offset in range(CONV):
        lower_row = CONV - 1 - offset
        keep = (extended_ids[lower_row : lower_row + tok_rows] == doc_ids).astype(jnp.float32)
        convolved = (
            convolved
            + taps[offset][None, :]
            * extended[lower_row : lower_row + tok_rows].astype(jnp.float32)
            * keep[:, None]
        )
    opening = jax.nn.sigmoid(gate.astype(jnp.float32))
    value_rows = (convolved * opening).astype(jnp.bfloat16)
    q_float = query.astype(jnp.float32).reshape(tok_rows, HEADS, KD)
    k_float = key.astype(jnp.float32).reshape(tok_rows, HEADS, KD)
    v_float = value_rows.astype(jnp.float32).reshape(tok_rows, HEADS, VD)
    scores = (
        jnp.einsum(
            "thd,shd->hts",
            query.reshape(tok_rows, HEADS, KD),
            key.reshape(tok_rows, HEADS, KD),
            preferred_element_type=jnp.float32,
        )
        * 0.25
    )
    kernel = 1.0 + scores + 0.5 * scores * scores
    allowed = (local_pos[:, None] >= local_pos[None, :]) & (doc_ids[:, None] == doc_ids[None, :])
    weights = jnp.where(allowed[None], kernel, 0.0)
    numerator = jnp.einsum("hts,shv->thv", weights, v_float, precision=high)
    denominator = jnp.transpose(jnp.sum(weights, axis=2), (1, 0))
    phi_query, spread_query = feature_rows(query.reshape(tok_rows, HEADS, KD))
    phi_key, spread_key = feature_rows(key.reshape(tok_rows, HEADS, KD))
    last_mask = (doc_ids == doc_ids[tok_rows - 1]).astype(jnp.float32)
    masked_key = phi_key * last_mask[None, None, :]
    local_state = jnp.einsum("hft,thv->hfv", masked_key, v_float, precision=high)
    local_norm = jnp.sum(masked_key, axis=2)
    restart_all, closes_all = block_flags(doc_lengths, lax.axis_size("ctx"), tok_rows)
    forward_mask, backward_mask = scan_masks(restart_all, closes_all)
    state_in, norm_in = state_scan(local_state, local_norm, forward_mask)
    inside = (doc_ids == prev_doc).astype(jnp.float32)
    numerator = numerator + inside[:, None, None] * jnp.einsum(
        "hft,hfv->thv", phi_query, state_in, precision=high
    )
    denominator = denominator + inside[:, None] * jnp.einsum(
        "hft,hf->th", phi_query, norm_in, precision=high
    )
    attended = numerator / denominator[:, :, None]
    mixed = attended.reshape(tok_rows, HEADS * VD).astype(jnp.bfloat16)
    upstream = d_out.astype(jnp.float32).reshape(tok_rows, HEADS, VD)
    grad_num = upstream / denominator[:, :, None]
    grad_den = -jnp.sum(upstream * attended, axis=2) / denominator
    first_mask = (doc_ids == doc_ids[0]).astype(jnp.float32)
    masked_query = phi_query * first_mask[None, None, :]
    back_state = jnp.einsum("hft,thv->hfv", masked_query, grad_num, precision=high)
    back_norm = jnp.einsum("hft,th->hf", masked_query, grad_den, precision=high)
    grad_state_in, grad_norm_in = state_scan(back_state, back_norm, backward_mask)
    outside = (doc_ids == next_doc).astype(jnp.float32)
    grad_v = jnp.einsum("hts,thv->shv", weights, grad_num, precision=high)
    grad_v = grad_v + outside[:, None, None] * jnp.einsum(
        "hfs,hfv->shv", phi_key, grad_state_in, precision=high
    )
    grad_weights = (
        jnp.einsum("thv,shv->hts", grad_num, v_float, precision=high)
        + jnp.transpose(grad_den, (1, 0))[:, :, None]
    )
    grad_scores = jnp.where(allowed[None], grad_weights * (1.0 + scores), 0.0)
    grad_q = jnp.einsum("hts,shd->thd", grad_scores, k_float, precision=high) * 0.25
    grad_k = jnp.einsum("hts,thd->shd", grad_scores, q_float, precision=high) * 0.25
    grad_phi_query = inside[None, None, :] * (
        jnp.einsum("hfv,thv->hft", state_in, grad_num, precision=high)
        + norm_in[:, :, None] * jnp.transpose(grad_den, (1, 0))[:, None, :]
    )
    grad_phi_key = outside[None, None, :] * (
        jnp.einsum("hfv,shv->hfs", grad_state_in, v_float, precision=high)
        + grad_norm_in[:, :, None]
    )
    grad_q = grad_q + feature_grad(grad_phi_query, spread_query)
    grad_k = grad_k + feature_grad(grad_phi_key, spread_key)
    grad_query = grad_q.reshape(tok_rows, HEADS * KD).astype(jnp.bfloat16)
    grad_key = grad_k.reshape(tok_rows, HEADS * KD).astype(jnp.bfloat16)
    grad_core = grad_v.reshape(tok_rows, channels)
    grad_gate = (grad_core * convolved * opening * (1.0 - opening)).astype(jnp.bfloat16)
    grad_conv = grad_core * opening
    later_rows = shifted(grad_conv[: CONV - 1], "ctx", -1)
    ahead = jnp.concatenate([grad_conv, later_rows], axis=0)
    ahead_ids = jnp.concatenate([doc_ids, after_ids], axis=0)
    grad_value = jnp.zeros((tok_rows, channels), jnp.float32)
    for offset in range(CONV):
        keep = (ahead_ids[offset : offset + tok_rows] == doc_ids).astype(jnp.float32)
        grad_value = (
            grad_value + taps[offset][None, :] * ahead[offset : offset + tok_rows] * keep[:, None]
        )
    return (mixed, grad_query, grad_key, grad_value.astype(jnp.bfloat16), grad_gate)


def solution(mesh):
    placed = (
        P(("dp", "ctx"), None),
        P(("dp", "ctx"), None),
        P(("dp", "ctx"), None),
        P(("dp", "ctx"), None),
        P(),
        P("dp"),
        P(("dp", "ctx"), None),
    )
    return jax.shard_map(
        local,
        mesh=mesh,
        in_specs=placed,
        out_specs=(
            P(("dp", "ctx"), None),
            P(("dp", "ctx"), None),
            P(("dp", "ctx"), None),
            P(("dp", "ctx"), None),
            P(("dp", "ctx"), None),
        ),
        check_vma=False,
    )
```

```python
import math

import jax
import numpy as np
import jax.numpy as jnp
from jax import lax
from jax.sharding import PartitionSpec as P

HEADS = 8
KD = 16
VD = 128
CONV = 3


highest = lax.Precision.HIGHEST
high = lax.Precision.HIGH
quad_scale = 1.0 / (4.0 * math.sqrt(2.0))


def shifted(block, axis, distance):
    devices = range(lax.axis_size(axis))
    route = [(i - distance, i) for i in devices if i - distance in devices]
    return lax.ppermute(block, axis, route)


def document_ids(lengths, positions):
    ends = jnp.cumsum(lengths, dtype=jnp.int32)
    counted = jnp.sum((ends[None, :] <= positions[:, None]).astype(jnp.int32), axis=1)
    return jnp.where(positions < 0, jnp.int32(-1), counted)


def pair_tables(width):
    rows, cols = np.triu_indices(width)
    quad_weight = np.where(rows == cols, quad_scale, quad_scale * math.sqrt(2.0))
    first = np.concatenate([[-1], np.full(width, -1), rows])
    second = np.concatenate([[-1], np.arange(width), cols])
    scale = np.concatenate([[1.0], np.full(width, 0.5), quad_weight]).astype(np.float32)
    feats = scale.size
    padded = -(-(feats + -(-feats // 128)) // 8) * 8
    extra = padded - feats
    first = np.concatenate([first, np.full(extra, width)])
    second = np.concatenate([second, np.full(extra, width)])
    scale = np.concatenate([scale, np.zeros(extra, np.float32)])
    dims = np.arange(width)
    pick_first = (first[:, None] == dims[None, :]).astype(np.float32)
    pick_second = (second[:, None] == dims[None, :]).astype(np.float32)
    return pick_first, (first < 0).astype(np.float32), pick_second, (second < 0).astype(np.float32), scale


def feature_rows(values):
    token_count, head_count, width = values.shape
    pick_first, one_first, pick_second, one_second, scale = pair_tables(width)
    picks = jnp.asarray(np.stack([pick_first, pick_second]), jnp.bfloat16)
    chosen = jnp.einsum("pfd,thd->phft", picks, values, preferred_element_type=jnp.float32)
    left = chosen[0] + jnp.asarray(one_first)[None, :, None]
    right = chosen[1] + jnp.asarray(one_second)[None, :, None]
    return (jnp.asarray(scale)[None, :, None] * left * right, (left, right))


def feature_grad(grad_phi, factors):
    left, right = factors
    width = 16
    pick_first, _, pick_second, _, scale = pair_tables(width)
    scaled = grad_phi * jnp.asarray(scale)[None, :, None]
    picks = jnp.asarray(np.concatenate([pick_first, pick_second], axis=0))
    both = jnp.concatenate([scaled * right, scaled * left], axis=1)
    return jnp.einsum("fd,hft->thd", picks, both, precision=high)


def block_flags(doc_lengths, devices, rows):
    firsts = jnp.arange(devices, dtype=jnp.int32) * rows
    prev_docs = document_ids(doc_lengths, firsts - 1)
    first_docs = document_ids(doc_lengths, firsts)
    last_docs = document_ids(doc_lengths, firsts + rows - 1)
    next_docs = document_ids(doc_lengths, firsts + rows)
    return (last_docs != prev_docs).astype(jnp.int32), (first_docs != next_docs).astype(jnp.int32)


def scan_masks(restart, closes):
    devices = restart.shape[0]
    order = jnp.arange(devices, dtype=jnp.int32)
    target = order[:, None]
    source = order[None, :]
    restarts_upto = jnp.cumsum(restart)
    closes_upto = jnp.cumsum(closes)
    gap_fwd = restarts_upto[jnp.maximum(target - 1, 0)] - restarts_upto[source]
    forward = (source < target) & (gap_fwd == 0)
    gap_bwd = closes_upto[jnp.maximum(source - 1, 0)] - closes_upto[target]
    backward = (source > target) & (gap_bwd == 0)
    return forward.astype(jnp.float32), backward.astype(jnp.float32)


def state_scan(local_state, local_norm, mask):
    devices = mask.shape[0]
    heads, feats, width = local_state.shape
    norm_rows = -(-feats // width)
    room = feats - norm_rows
    norm_block = jnp.pad(local_norm, ((0, 0), (0, norm_rows * width - feats)))
    packed = lax.dynamic_update_slice(
        local_state, norm_block.reshape(heads, norm_rows, width), (0, room, 0)
    ).reshape(devices, -1, width)
    chunks = lax.all_to_all(packed, "ctx", 0, 0, tiled=True)
    summed = jnp.einsum("ij,jrc->irc", mask, chunks, precision=high)
    back = lax.all_to_all(summed, "ctx", 0, 0, tiled=True).reshape(heads, feats, width)
    norm_in = back[:, room:].reshape(heads, norm_rows * width)[:, :feats]
    return (back, norm_in)


def local(query, key, value_in, gate, conv_weight, doc_lengths, d_out):
    tok_rows = query.shape[0]
    channels = value_in.shape[1]
    dev_index = lax.axis_index("ctx")
    first_pos = dev_index * tok_rows
    local_pos = jnp.arange(tok_rows, dtype=jnp.int32)
    doc_ids = document_ids(doc_lengths, first_pos + local_pos)
    edge_docs = document_ids(doc_lengths, first_pos + jnp.array([-1, tok_rows], jnp.int32))
    prev_doc = edge_docs[0]
    next_doc = edge_docs[1]
    before_ids = document_ids(
        doc_lengths, first_pos - (CONV - 1) + jnp.arange(CONV - 1, dtype=jnp.int32)
    )
    after_ids = document_ids(
        doc_lengths, first_pos + tok_rows + jnp.arange(CONV - 1, dtype=jnp.int32)
    )
    taps = conv_weight.astype(jnp.float32)
    earlier = shifted(value_in[tok_rows - (CONV - 1) :], "ctx", 1)
    extended = jnp.concatenate([earlier, value_in], axis=0)
    extended_ids = jnp.concatenate([before_ids, doc_ids], axis=0)
    convolved = jnp.zeros((tok_rows, channels), jnp.float32)
    for offset in range(CONV):
        lower_row = CONV - 1 - offset
        keep = (extended_ids[lower_row : lower_row + tok_rows] == doc_ids).astype(jnp.float32)
        convolved = (
            convolved
            + taps[offset][None, :]
            * extended[lower_row : lower_row + tok_rows].astype(jnp.float32)
            * keep[:, None]
        )
    opening = jax.nn.sigmoid(gate.astype(jnp.float32))
    value_rows = (convolved * opening).astype(jnp.bfloat16)
    q_float = query.astype(jnp.float32).reshape(tok_rows, HEADS, KD)
    k_float = key.astype(jnp.float32).reshape(tok_rows, HEADS, KD)
    v_float = value_rows.astype(jnp.float32).reshape(tok_rows, HEADS, VD)
    scores = (
        jnp.einsum(
            "thd,shd->hts",
            query.reshape(tok_rows, HEADS, KD),
            key.reshape(tok_rows, HEADS, KD),
            preferred_element_type=jnp.float32,
        )
        * 0.25
    )
    kernel = 1.0 + scores + 0.5 * scores * scores
    allowed = (local_pos[:, None] >= local_pos[None, :]) & (doc_ids[:, None] == doc_ids[None, :])
    weights = jnp.where(allowed[None], kernel, 0.0)
    numerator = jnp.einsum("hts,shv->thv", weights, v_float, precision=high)
    denominator = jnp.transpose(jnp.sum(weights, axis=2), (1, 0))
    phi_query, spread_query = feature_rows(query.reshape(tok_rows, HEADS, KD))
    phi_key, spread_key = feature_rows(key.reshape(tok_rows, HEADS, KD))
    last_mask = (doc_ids == doc_ids[tok_rows - 1]).astype(jnp.float32)
    masked_key = phi_key * last_mask[None, None, :]
    local_state = jnp.einsum("hft,thv->hfv", masked_key, v_float, precision=high)
    local_norm = jnp.sum(masked_key, axis=2)
    restart_all, closes_all = block_flags(doc_lengths, lax.axis_size("ctx"), tok_rows)
    forward_mask, backward_mask = scan_masks(restart_all, closes_all)
    state_in, norm_in = state_scan(local_state, local_norm, forward_mask)
    inside = (doc_ids == prev_doc).astype(jnp.float32)
    numerator = numerator + inside[:, None, None] * jnp.einsum(
        "hft,hfv->thv", phi_query, state_in, precision=high
    )
    denominator = denominator + inside[:, None] * jnp.einsum(
        "hft,hf->th", phi_query, norm_in, precision=high
    )
    attended = numerator / denominator[:, :, None]
    mixed = attended.reshape(tok_rows, HEADS * VD).astype(jnp.bfloat16)
    upstream = d_out.astype(jnp.float32).reshape(tok_rows, HEADS, VD)
    grad_num = upstream / denominator[:, :, None]
    grad_den = -jnp.sum(upstream * attended, axis=2) / denominator
    first_mask = (doc_ids == doc_ids[0]).astype(jnp.float32)
    masked_query = phi_query * first_mask[None, None, :]
    back_state = jnp.einsum("hft,thv->hfv", masked_query, grad_num, precision=high)
    back_norm = jnp.einsum("hft,th->hf", masked_query, grad_den, precision=high)
    grad_state_in, grad_norm_in = state_scan(back_state, back_norm, backward_mask)
    outside = (doc_ids == next_doc).astype(jnp.float32)
    grad_v = jnp.einsum("hts,thv->shv", weights, grad_num, precision=high)
    grad_v = grad_v + outside[:, None, None] * jnp.einsum(
        "hfs,hfv->shv", phi_key, grad_state_in, precision=high
    )
    grad_weights = (
        jnp.einsum("thv,shv->hts", grad_num, v_float, precision=high)
        + jnp.transpose(grad_den, (1, 0))[:, :, None]
    )
    grad_scores = jnp.where(allowed[None], grad_weights * (1.0 + scores), 0.0)
    grad_q = jnp.einsum("hts,shd->thd", grad_scores, k_float, precision=high) * 0.25
    grad_k = jnp.einsum("hts,thd->shd", grad_scores, q_float, precision=high) * 0.25
    grad_phi_query = inside[None, None, :] * (
        jnp.einsum("hfv,thv->hft", state_in, grad_num, precision=high)
        + norm_in[:, :, None] * jnp.transpose(grad_den, (1, 0))[:, None, :]
    )
    grad_phi_key = outside[None, None, :] * (
        jnp.einsum("hfv,shv->hfs", grad_state_in, v_float, precision=high)
        + grad_norm_in[:, :, None]
    )
    grad_q = grad_q + feature_grad(grad_phi_query, spread_query)
    grad_k = grad_k + feature_grad(grad_phi_key, spread_key)
    grad_query = grad_q.reshape(tok_rows, HEADS * KD).astype(jnp.bfloat16)
    grad_key = grad_k.reshape(tok_rows, HEADS * KD).astype(jnp.bfloat16)
    grad_core = grad_v.reshape(tok_rows, channels)
    grad_gate = (grad_core * convolved * opening * (1.0 - opening)).astype(jnp.bfloat16)
    grad_conv = grad_core * opening
    later_rows = shifted(grad_conv[: CONV - 1], "ctx", -1)
    ahead = jnp.concatenate([grad_conv, later_rows], axis=0)
    ahead_ids = jnp.concatenate([doc_ids, after_ids], axis=0)
    grad_value = jnp.zeros((tok_rows, channels), jnp.float32)
    for offset in range(CONV):
        keep = (ahead_ids[offset : offset + tok_rows] == doc_ids).astype(jnp.float32)
        grad_value = (
            grad_value + taps[offset][None, :] * ahead[offset : offset + tok_rows] * keep[:, None]
        )
    return (mixed, grad_query, grad_key, grad_value.astype(jnp.bfloat16), grad_gate)


def solution(mesh):
    placed = (
        P(("dp", "ctx"), None),
        P(("dp", "ctx"), None),
        P(("dp", "ctx"), None),
        P(("dp", "ctx"), None),
        P(),
        P("dp"),
        P(("dp", "ctx"), None),
    )
    return jax.shard_map(
        local,
        mesh=mesh,
        in_specs=placed,
        out_specs=(
            P(("dp", "ctx"), None),
            P(("dp", "ctx"), None),
            P(("dp", "ctx"), None),
            P(("dp", "ctx"), None),
            P(("dp", "ctx"), None),
        ),
        check_vma=False,
    )
```

```python
import math

import jax
import numpy as np
import jax.numpy as jnp
from jax import lax
from jax.sharding import PartitionSpec as P

HEADS = 8
KD = 16
VD = 128
CONV = 3


highest = lax.Precision.HIGHEST
high = lax.Precision.HIGH
quad_scale = 1.0 / (4.0 * math.sqrt(2.0))


def shifted(block, axis, distance):
    devices = range(lax.axis_size(axis))
    route = [(i - distance, i) for i in devices if i - distance in devices]
    return lax.ppermute(block, axis, route)


def document_ids(lengths, positions):
    ends = jnp.cumsum(lengths, dtype=jnp.int32)
    counted = jnp.sum((ends[None, :] <= positions[:, None]).astype(jnp.int32), axis=1)
    return jnp.where(positions < 0, jnp.int32(-1), counted)


def pair_tables(width):
    rows, cols = np.triu_indices(width)
    quad_weight = np.where(rows == cols, quad_scale, quad_scale * math.sqrt(2.0))
    first = np.concatenate([[-1], np.full(width, -1), rows])
    second = np.concatenate([[-1], np.arange(width), cols])
    scale = np.concatenate([[1.0], np.full(width, 0.5), quad_weight]).astype(np.float32)
    feats = scale.size
    padded = -(-(feats + -(-feats // 128)) // 8) * 8
    extra = padded - feats
    first = np.concatenate([first, np.full(extra, width)])
    second = np.concatenate([second, np.full(extra, width)])
    scale = np.concatenate([scale, np.zeros(extra, np.float32)])
    dims = np.arange(width)
    pick_first = (first[:, None] == dims[None, :]).astype(np.float32)
    pick_second = (second[:, None] == dims[None, :]).astype(np.float32)
    return pick_first, (first < 0).astype(np.float32), pick_second, (second < 0).astype(np.float32), scale


def feature_rows(values):
    token_count, head_count, width = values.shape
    pick_first, one_first, pick_second, one_second, scale = pair_tables(width)
    picks = jnp.asarray(np.stack([pick_first, pick_second]), jnp.bfloat16)
    chosen = jnp.einsum("pfd,thd->phft", picks, values, preferred_element_type=jnp.float32)
    left = chosen[0] + jnp.asarray(one_first)[None, :, None]
    right = chosen[1] + jnp.asarray(one_second)[None, :, None]
    return (jnp.asarray(scale)[None, :, None] * left * right, (left, right))


def feature_grad(grad_phi, factors):
    left, right = factors
    width = 16
    pick_first, _, pick_second, _, scale = pair_tables(width)
    scaled = grad_phi * jnp.asarray(scale)[None, :, None]
    picks = jnp.asarray(np.concatenate([pick_first, pick_second], axis=0))
    both = jnp.concatenate([scaled * right, scaled * left], axis=1)
    return jnp.einsum("fd,hft->thd", picks, both, precision=high)


def block_flags(doc_lengths, devices, rows):
    firsts = jnp.arange(devices, dtype=jnp.int32) * rows
    prev_docs = document_ids(doc_lengths, firsts - 1)
    first_docs = document_ids(doc_lengths, firsts)
    last_docs = document_ids(doc_lengths, firsts + rows - 1)
    next_docs = document_ids(doc_lengths, firsts + rows)
    return (last_docs != prev_docs).astype(jnp.int32), (first_docs != next_docs).astype(jnp.int32)


def scan_masks(restart, closes):
    devices = restart.shape[0]
    order = jnp.arange(devices, dtype=jnp.int32)
    target = order[:, None]
    source = order[None, :]
    restarts_upto = jnp.cumsum(restart)
    closes_upto = jnp.cumsum(closes)
    gap_fwd = restarts_upto[jnp.maximum(target - 1, 0)] - restarts_upto[source]
    forward = (source < target) & (gap_fwd == 0)
    gap_bwd = closes_upto[jnp.maximum(source - 1, 0)] - closes_upto[target]
    backward = (source > target) & (gap_bwd == 0)
    return forward.astype(jnp.float32), backward.astype(jnp.float32)


def state_scan(local_state, local_norm, mask, filler):
    devices = mask.shape[0]
    heads, feats, width = local_state.shape
    norm_rows = -(-feats // width)
    room = feats - norm_rows
    norm_block = jnp.pad(local_norm, ((0, 0), (0, norm_rows * width - feats)))
    packed = lax.dynamic_update_slice(
        local_state, norm_block.reshape(heads, norm_rows, width), (0, room, 0)
    ).reshape(devices, -1, width)
    chunks = lax.all_to_all(packed, "ctx", 0, 0, tiled=True)
    chunks, filler = lax.optimization_barrier((chunks, filler))
    summed = jnp.einsum("ij,jrc->irc", mask, chunks, precision=high)
    back = lax.all_to_all(summed, "ctx", 0, 0, tiled=True).reshape(heads, feats, width)
    norm_in = back[:, room:].reshape(heads, norm_rows * width)[:, :feats]
    return (back, norm_in, filler)


def local(query, key, value_in, gate, conv_weight, doc_lengths, d_out):
    tok_rows = query.shape[0]
    channels = value_in.shape[1]
    dev_index = lax.axis_index("ctx")
    first_pos = dev_index * tok_rows
    local_pos = jnp.arange(tok_rows, dtype=jnp.int32)
    doc_ids = document_ids(doc_lengths, first_pos + local_pos)
    edge_docs = document_ids(doc_lengths, first_pos + jnp.array([-1, tok_rows], jnp.int32))
    prev_doc = edge_docs[0]
    next_doc = edge_docs[1]
    before_ids = document_ids(
        doc_lengths, first_pos - (CONV - 1) + jnp.arange(CONV - 1, dtype=jnp.int32)
    )
    after_ids = document_ids(
        doc_lengths, first_pos + tok_rows + jnp.arange(CONV - 1, dtype=jnp.int32)
    )
    taps = conv_weight.astype(jnp.float32)
    earlier = shifted(value_in[tok_rows - (CONV - 1) :], "ctx", 1)
    extended = jnp.concatenate([earlier, value_in], axis=0)
    extended_ids = jnp.concatenate([before_ids, doc_ids], axis=0)
    convolved = jnp.zeros((tok_rows, channels), jnp.float32)
    for offset in range(CONV):
        lower_row = CONV - 1 - offset
        keep = (extended_ids[lower_row : lower_row + tok_rows] == doc_ids).astype(jnp.float32)
        convolved = (
            convolved
            + taps[offset][None, :]
            * extended[lower_row : lower_row + tok_rows].astype(jnp.float32)
            * keep[:, None]
        )
    opening = jax.nn.sigmoid(gate.astype(jnp.float32))
    value_rows = (convolved * opening).astype(jnp.bfloat16)
    q_float = query.astype(jnp.float32).reshape(tok_rows, HEADS, KD)
    k_float = key.astype(jnp.float32).reshape(tok_rows, HEADS, KD)
    v_float = value_rows.astype(jnp.float32).reshape(tok_rows, HEADS, VD)
    scores = (
        jnp.einsum(
            "thd,shd->hts",
            query.reshape(tok_rows, HEADS, KD),
            key.reshape(tok_rows, HEADS, KD),
            preferred_element_type=jnp.float32,
        )
        * 0.25
    )
    kernel = 1.0 + scores + 0.5 * scores * scores
    allowed = (local_pos[:, None] >= local_pos[None, :]) & (doc_ids[:, None] == doc_ids[None, :])
    weights = jnp.where(allowed[None], kernel, 0.0)
    numerator = jnp.einsum("hts,shv->thv", weights, v_float, precision=high)
    denominator = jnp.transpose(jnp.sum(weights, axis=2), (1, 0))
    phi_query, spread_query = feature_rows(query.reshape(tok_rows, HEADS, KD))
    phi_key, spread_key = feature_rows(key.reshape(tok_rows, HEADS, KD))
    last_mask = (doc_ids == doc_ids[tok_rows - 1]).astype(jnp.float32)
    masked_key = phi_key * last_mask[None, None, :]
    local_state = jnp.einsum("hft,thv->hfv", masked_key, v_float, precision=high)
    local_norm = jnp.sum(masked_key, axis=2)
    restart_all, closes_all = block_flags(doc_lengths, lax.axis_size("ctx"), tok_rows)
    forward_mask, backward_mask = scan_masks(restart_all, closes_all)
    state_in, norm_in, (numerator, denominator) = state_scan(
        local_state, local_norm, forward_mask, (numerator, denominator)
    )
    inside = (doc_ids == prev_doc).astype(jnp.float32)
    numerator = numerator + inside[:, None, None] * jnp.einsum(
        "hft,hfv->thv", phi_query, state_in, precision=high
    )
    denominator = denominator + inside[:, None] * jnp.einsum(
        "hft,hf->th", phi_query, norm_in, precision=high
    )
    attended = numerator / denominator[:, :, None]
    mixed = attended.reshape(tok_rows, HEADS * VD).astype(jnp.bfloat16)
    upstream = d_out.astype(jnp.float32).reshape(tok_rows, HEADS, VD)
    grad_num = upstream / denominator[:, :, None]
    grad_den = -jnp.sum(upstream * attended, axis=2) / denominator
    first_mask = (doc_ids == doc_ids[0]).astype(jnp.float32)
    masked_query = phi_query * first_mask[None, None, :]
    back_state = jnp.einsum("hft,thv->hfv", masked_query, grad_num, precision=high)
    back_norm = jnp.einsum("hft,th->hf", masked_query, grad_den, precision=high)
    outside = (doc_ids == next_doc).astype(jnp.float32)
    grad_v = jnp.einsum("hts,thv->shv", weights, grad_num, precision=high)
    grad_weights = (
        jnp.einsum("thv,shv->hts", grad_num, v_float, precision=high)
        + jnp.transpose(grad_den, (1, 0))[:, :, None]
    )
    grad_scores = jnp.where(allowed[None], grad_weights * (1.0 + scores), 0.0)
    grad_q = jnp.einsum("hts,shd->thd", grad_scores, k_float, precision=high) * 0.25
    grad_k = jnp.einsum("hts,thd->shd", grad_scores, q_float, precision=high) * 0.25
    grad_phi_query = inside[None, None, :] * (
        jnp.einsum("hfv,thv->hft", state_in, grad_num, precision=high)
        + norm_in[:, :, None] * jnp.transpose(grad_den, (1, 0))[:, None, :]
    )
    grad_q = grad_q + feature_grad(grad_phi_query, spread_query)
    grad_state_in, grad_norm_in, (grad_v, grad_q, grad_k) = state_scan(
        back_state, back_norm, backward_mask, (grad_v, grad_q, grad_k)
    )
    grad_v = grad_v + outside[:, None, None] * jnp.einsum(
        "hfs,hfv->shv", phi_key, grad_state_in, precision=high
    )
    grad_phi_key = outside[None, None, :] * (
        jnp.einsum("hfv,shv->hfs", grad_state_in, v_float, precision=high)
        + grad_norm_in[:, :, None]
    )
    grad_k = grad_k + feature_grad(grad_phi_key, spread_key)
    grad_query = grad_q.reshape(tok_rows, HEADS * KD).astype(jnp.bfloat16)
    grad_key = grad_k.reshape(tok_rows, HEADS * KD).astype(jnp.bfloat16)
    grad_core = grad_v.reshape(tok_rows, channels)
    grad_gate = (grad_core * convolved * opening * (1.0 - opening)).astype(jnp.bfloat16)
    grad_conv = grad_core * opening
    later_rows = shifted(grad_conv[: CONV - 1], "ctx", -1)
    ahead = jnp.concatenate([grad_conv, later_rows], axis=0)
    ahead_ids = jnp.concatenate([doc_ids, after_ids], axis=0)
    grad_value = jnp.zeros((tok_rows, channels), jnp.float32)
    for offset in range(CONV):
        keep = (ahead_ids[offset : offset + tok_rows] == doc_ids).astype(jnp.float32)
        grad_value = (
            grad_value + taps[offset][None, :] * ahead[offset : offset + tok_rows] * keep[:, None]
        )
    return (mixed, grad_query, grad_key, grad_value.astype(jnp.bfloat16), grad_gate)


def solution(mesh):
    placed = (
        P(("dp", "ctx"), None),
        P(("dp", "ctx"), None),
        P(("dp", "ctx"), None),
        P(("dp", "ctx"), None),
        P(),
        P("dp"),
        P(("dp", "ctx"), None),
    )
    return jax.shard_map(
        local,
        mesh=mesh,
        in_specs=placed,
        out_specs=(
            P(("dp", "ctx"), None),
            P(("dp", "ctx"), None),
            P(("dp", "ctx"), None),
            P(("dp", "ctx"), None),
            P(("dp", "ctx"), None),
        ),
        check_vma=False,
    )
```

```python
import math

import jax
import numpy as np
import jax.numpy as jnp
from jax import lax
from jax.sharding import PartitionSpec as P

HEADS = 8
KD = 16
VD = 128
CONV = 3


highest = lax.Precision.HIGHEST
high = lax.Precision.HIGH
quad_scale = 1.0 / (4.0 * math.sqrt(2.0))


def shifted(block, axis, distance):
    devices = range(lax.axis_size(axis))
    route = [(i - distance, i) for i in devices if i - distance in devices]
    return lax.ppermute(block, axis, route)


def document_ids(lengths, positions):
    ends = jnp.cumsum(lengths, dtype=jnp.int32)
    counted = jnp.sum((ends[None, :] <= positions[:, None]).astype(jnp.int32), axis=1)
    return jnp.where(positions < 0, jnp.int32(-1), counted)


def pair_tables(width):
    rows, cols = np.triu_indices(width)
    quad_weight = np.where(rows == cols, quad_scale, quad_scale * math.sqrt(2.0))
    first = np.concatenate([[-1], np.full(width, -1), rows])
    second = np.concatenate([[-1], np.arange(width), cols])
    scale = np.concatenate([[1.0], np.full(width, 0.5), quad_weight]).astype(np.float32)
    feats = scale.size
    padded = -(-(feats + -(-feats // 128)) // 8) * 8
    extra = padded - feats
    first = np.concatenate([first, np.full(extra, width)])
    second = np.concatenate([second, np.full(extra, width)])
    scale = np.concatenate([scale, np.zeros(extra, np.float32)])
    dims = np.arange(width)
    pick_first = (first[:, None] == dims[None, :]).astype(np.float32)
    pick_second = (second[:, None] == dims[None, :]).astype(np.float32)
    return pick_first, (first < 0).astype(np.float32), pick_second, (second < 0).astype(np.float32), scale


def feature_rows(values):
    token_count, head_count, width = values.shape
    pick_first, one_first, pick_second, one_second, scale = pair_tables(width)
    picks = jnp.asarray(np.stack([pick_first, pick_second]), jnp.bfloat16)
    chosen = jnp.einsum("pfd,thd->phft", picks, values, preferred_element_type=jnp.float32)
    left = chosen[0] + jnp.asarray(one_first)[None, :, None]
    right = chosen[1] + jnp.asarray(one_second)[None, :, None]
    return (jnp.asarray(scale)[None, :, None] * left * right, (left, right))


def feature_grad(grad_phi, factors):
    left, right = factors
    width = 16
    pick_first, _, pick_second, _, scale = pair_tables(width)
    scaled = grad_phi * jnp.asarray(scale)[None, :, None]
    picks = jnp.asarray(np.concatenate([pick_first, pick_second], axis=0))
    both = jnp.concatenate([scaled * right, scaled * left], axis=1)
    return jnp.einsum("fd,hft->thd", picks, both, precision=high)


def block_flags(doc_lengths, devices, rows):
    firsts = jnp.arange(devices, dtype=jnp.int32) * rows
    prev_docs = document_ids(doc_lengths, firsts - 1)
    first_docs = document_ids(doc_lengths, firsts)
    last_docs = document_ids(doc_lengths, firsts + rows - 1)
    next_docs = document_ids(doc_lengths, firsts + rows)
    return (last_docs != prev_docs).astype(jnp.int32), (first_docs != next_docs).astype(jnp.int32)


def scan_masks(restart, closes):
    devices = restart.shape[0]
    order = jnp.arange(devices, dtype=jnp.int32)
    target = order[:, None]
    source = order[None, :]
    restarts_upto = jnp.cumsum(restart)
    closes_upto = jnp.cumsum(closes)
    gap_fwd = restarts_upto[jnp.maximum(target - 1, 0)] - restarts_upto[source]
    forward = (source < target) & (gap_fwd == 0)
    gap_bwd = closes_upto[jnp.maximum(source - 1, 0)] - closes_upto[target]
    backward = (source > target) & (gap_bwd == 0)
    return forward.astype(jnp.float32), backward.astype(jnp.float32)


def state_scan(local_state, local_norm, mask, filler, later_filler):
    devices = mask.shape[0]
    heads, feats, width = local_state.shape
    norm_rows = -(-feats // width)
    room = feats - norm_rows
    norm_block = jnp.pad(local_norm, ((0, 0), (0, norm_rows * width - feats)))
    packed = lax.dynamic_update_slice(
        local_state, norm_block.reshape(heads, norm_rows, width), (0, room, 0)
    ).reshape(devices, -1, width)
    chunks = lax.all_to_all(packed, "ctx", 0, 0, tiled=True)
    chunks, filler = lax.optimization_barrier((chunks, filler))
    summed = jnp.einsum("ij,jrc->irc", mask, chunks, precision=high)
    back = lax.all_to_all(summed, "ctx", 0, 0, tiled=True)
    back, later_filler = lax.optimization_barrier((back, later_filler))
    back = back.reshape(heads, feats, width)
    norm_in = back[:, room:].reshape(heads, norm_rows * width)[:, :feats]
    return (back, norm_in, filler, later_filler)


def local(query, key, value_in, gate, conv_weight, doc_lengths, d_out):
    tok_rows = query.shape[0]
    channels = value_in.shape[1]
    dev_index = lax.axis_index("ctx")
    first_pos = dev_index * tok_rows
    local_pos = jnp.arange(tok_rows, dtype=jnp.int32)
    doc_ids = document_ids(doc_lengths, first_pos + local_pos)
    edge_docs = document_ids(doc_lengths, first_pos + jnp.array([-1, tok_rows], jnp.int32))
    prev_doc = edge_docs[0]
    next_doc = edge_docs[1]
    before_ids = document_ids(
        doc_lengths, first_pos - (CONV - 1) + jnp.arange(CONV - 1, dtype=jnp.int32)
    )
    after_ids = document_ids(
        doc_lengths, first_pos + tok_rows + jnp.arange(CONV - 1, dtype=jnp.int32)
    )
    taps = conv_weight.astype(jnp.float32)
    earlier = shifted(value_in[tok_rows - (CONV - 1) :], "ctx", 1)
    extended = jnp.concatenate([earlier, value_in], axis=0)
    extended_ids = jnp.concatenate([before_ids, doc_ids], axis=0)
    convolved = jnp.zeros((tok_rows, channels), jnp.float32)
    for offset in range(CONV):
        lower_row = CONV - 1 - offset
        keep = (extended_ids[lower_row : lower_row + tok_rows] == doc_ids).astype(jnp.float32)
        convolved = (
            convolved
            + taps[offset][None, :]
            * extended[lower_row : lower_row + tok_rows].astype(jnp.float32)
            * keep[:, None]
        )
    opening = jax.nn.sigmoid(gate.astype(jnp.float32))
    value_rows = (convolved * opening).astype(jnp.bfloat16)
    q_float = query.astype(jnp.float32).reshape(tok_rows, HEADS, KD)
    k_float = key.astype(jnp.float32).reshape(tok_rows, HEADS, KD)
    v_float = value_rows.astype(jnp.float32).reshape(tok_rows, HEADS, VD)
    scores = (
        jnp.einsum(
            "thd,shd->hts",
            query.reshape(tok_rows, HEADS, KD),
            key.reshape(tok_rows, HEADS, KD),
            preferred_element_type=jnp.float32,
        )
        * 0.25
    )
    kernel = 1.0 + scores + 0.5 * scores * scores
    allowed = (local_pos[:, None] >= local_pos[None, :]) & (doc_ids[:, None] == doc_ids[None, :])
    weights = jnp.where(allowed[None], kernel, 0.0)
    numerator = jnp.einsum("hts,shv->thv", weights, v_float, precision=high)
    denominator = jnp.transpose(jnp.sum(weights, axis=2), (1, 0))
    phi_query, spread_query = feature_rows(query.reshape(tok_rows, HEADS, KD))
    phi_key, spread_key = feature_rows(key.reshape(tok_rows, HEADS, KD))
    last_mask = (doc_ids == doc_ids[tok_rows - 1]).astype(jnp.float32)
    masked_key = phi_key * last_mask[None, None, :]
    local_state = jnp.einsum("hft,thv->hfv", masked_key, v_float, precision=high)
    local_norm = jnp.sum(masked_key, axis=2)
    restart_all, closes_all = block_flags(doc_lengths, lax.axis_size("ctx"), tok_rows)
    forward_mask, backward_mask = scan_masks(restart_all, closes_all)
    state_in, norm_in, (numerator, denominator), _ = state_scan(
        local_state, local_norm, forward_mask, (numerator, denominator), ()
    )
    inside = (doc_ids == prev_doc).astype(jnp.float32)
    numerator = numerator + inside[:, None, None] * jnp.einsum(
        "hft,hfv->thv", phi_query, state_in, precision=high
    )
    denominator = denominator + inside[:, None] * jnp.einsum(
        "hft,hf->th", phi_query, norm_in, precision=high
    )
    attended = numerator / denominator[:, :, None]
    mixed = attended.reshape(tok_rows, HEADS * VD).astype(jnp.bfloat16)
    upstream = d_out.astype(jnp.float32).reshape(tok_rows, HEADS, VD)
    grad_num = upstream / denominator[:, :, None]
    grad_den = -jnp.sum(upstream * attended, axis=2) / denominator
    first_mask = (doc_ids == doc_ids[0]).astype(jnp.float32)
    masked_query = phi_query * first_mask[None, None, :]
    back_state = jnp.einsum("hft,thv->hfv", masked_query, grad_num, precision=high)
    back_norm = jnp.einsum("hft,th->hf", masked_query, grad_den, precision=high)
    outside = (doc_ids == next_doc).astype(jnp.float32)
    grad_v = jnp.einsum("hts,thv->shv", weights, grad_num, precision=high)
    grad_weights = (
        jnp.einsum("thv,shv->hts", grad_num, v_float, precision=high)
        + jnp.transpose(grad_den, (1, 0))[:, :, None]
    )
    grad_scores = jnp.where(allowed[None], grad_weights * (1.0 + scores), 0.0)
    grad_q = jnp.einsum("hts,shd->thd", grad_scores, k_float, precision=high) * 0.25
    grad_k = jnp.einsum("hts,thd->shd", grad_scores, q_float, precision=high) * 0.25
    grad_phi_query = inside[None, None, :] * (
        jnp.einsum("hfv,thv->hft", state_in, grad_num, precision=high)
        + norm_in[:, :, None] * jnp.transpose(grad_den, (1, 0))[:, None, :]
    )
    grad_state_in, grad_norm_in, (grad_v, grad_q, grad_k), grad_q_tail = state_scan(
        back_state, back_norm, backward_mask, (grad_v, grad_q, grad_k), feature_grad(grad_phi_query, spread_query)
    )
    grad_q = grad_q + grad_q_tail
    grad_v = grad_v + outside[:, None, None] * jnp.einsum(
        "hfs,hfv->shv", phi_key, grad_state_in, precision=high
    )
    grad_phi_key = outside[None, None, :] * (
        jnp.einsum("hfv,shv->hfs", grad_state_in, v_float, precision=high)
        + grad_norm_in[:, :, None]
    )
    grad_k = grad_k + feature_grad(grad_phi_key, spread_key)
    grad_query = grad_q.reshape(tok_rows, HEADS * KD).astype(jnp.bfloat16)
    grad_key = grad_k.reshape(tok_rows, HEADS * KD).astype(jnp.bfloat16)
    grad_core = grad_v.reshape(tok_rows, channels)
    grad_gate = (grad_core * convolved * opening * (1.0 - opening)).astype(jnp.bfloat16)
    grad_conv = grad_core * opening
    later_rows = shifted(grad_conv[: CONV - 1], "ctx", -1)
    ahead = jnp.concatenate([grad_conv, later_rows], axis=0)
    ahead_ids = jnp.concatenate([doc_ids, after_ids], axis=0)
    grad_value = jnp.zeros((tok_rows, channels), jnp.float32)
    for offset in range(CONV):
        keep = (ahead_ids[offset : offset + tok_rows] == doc_ids).astype(jnp.float32)
        grad_value = (
            grad_value + taps[offset][None, :] * ahead[offset : offset + tok_rows] * keep[:, None]
        )
    return (mixed, grad_query, grad_key, grad_value.astype(jnp.bfloat16), grad_gate)


def solution(mesh):
    placed = (
        P(("dp", "ctx"), None),
        P(("dp", "ctx"), None),
        P(("dp", "ctx"), None),
        P(("dp", "ctx"), None),
        P(),
        P("dp"),
        P(("dp", "ctx"), None),
    )
    return jax.shard_map(
        local,
        mesh=mesh,
        in_specs=placed,
        out_specs=(
            P(("dp", "ctx"), None),
            P(("dp", "ctx"), None),
            P(("dp", "ctx"), None),
            P(("dp", "ctx"), None),
            P(("dp", "ctx"), None),
        ),
        check_vma=False,
    )
```

```python
import math

import jax
import numpy as np
import jax.numpy as jnp
from jax import lax
from jax.sharding import PartitionSpec as P

HEADS = 8
KD = 16
VD = 128
CONV = 3


highest = lax.Precision.HIGHEST
high = lax.Precision.HIGH
quad_scale = 1.0 / (4.0 * math.sqrt(2.0))


def shifted(block, axis, distance):
    devices = range(lax.axis_size(axis))
    route = [(i - distance, i) for i in devices if i - distance in devices]
    return lax.ppermute(block, axis, route)


def document_ids(lengths, positions):
    ends = jnp.cumsum(lengths, dtype=jnp.int32)
    counted = jnp.sum((ends[None, :] <= positions[:, None]).astype(jnp.int32), axis=1)
    return jnp.where(positions < 0, jnp.int32(-1), counted)


def pair_tables(width):
    rows, cols = np.triu_indices(width)
    quad_weight = np.where(rows == cols, quad_scale, quad_scale * math.sqrt(2.0))
    first = np.concatenate([[-1], np.full(width, -1), rows])
    second = np.concatenate([[-1], np.arange(width), cols])
    scale = np.concatenate([[1.0], np.full(width, 0.5), quad_weight]).astype(np.float32)
    feats = scale.size
    padded = -(-(feats + -(-feats // 128)) // 8) * 8
    extra = padded - feats
    first = np.concatenate([first, np.full(extra, width)])
    second = np.concatenate([second, np.full(extra, width)])
    scale = np.concatenate([scale, np.zeros(extra, np.float32)])
    dims = np.arange(width)
    pick_first = (first[:, None] == dims[None, :]).astype(np.float32)
    pick_second = (second[:, None] == dims[None, :]).astype(np.float32)
    return pick_first, (first < 0).astype(np.float32), pick_second, (second < 0).astype(np.float32), scale


def feature_rows(values):
    token_count, head_count, width = values.shape
    pick_first, one_first, pick_second, one_second, scale = pair_tables(width)
    picks = jnp.asarray(np.stack([pick_first, pick_second]), jnp.bfloat16)
    chosen = jnp.einsum("pfd,thd->phft", picks, values, preferred_element_type=jnp.float32)
    left = chosen[0] + jnp.asarray(one_first)[None, :, None]
    right = chosen[1] + jnp.asarray(one_second)[None, :, None]
    return (jnp.asarray(scale)[None, :, None] * left * right, (left, right))


def feature_grad(grad_phi, factors):
    left, right = factors
    width = 16
    pick_first, _, pick_second, _, scale = pair_tables(width)
    scaled = grad_phi * jnp.asarray(scale)[None, :, None]
    picks = jnp.asarray(np.concatenate([pick_first, pick_second], axis=0))
    both = jnp.concatenate([scaled * right, scaled * left], axis=1)
    return jnp.einsum("fd,hft->thd", picks, both, precision=high)


def block_flags(doc_lengths, devices, rows):
    firsts = jnp.arange(devices, dtype=jnp.int32) * rows
    prev_docs = document_ids(doc_lengths, firsts - 1)
    first_docs = document_ids(doc_lengths, firsts)
    last_docs = document_ids(doc_lengths, firsts + rows - 1)
    next_docs = document_ids(doc_lengths, firsts + rows)
    return (last_docs != prev_docs).astype(jnp.int32), (first_docs != next_docs).astype(jnp.int32)


def scan_masks(restart, closes):
    devices = restart.shape[0]
    order = jnp.arange(devices, dtype=jnp.int32)
    target = order[:, None]
    source = order[None, :]
    restarts_upto = jnp.cumsum(restart)
    closes_upto = jnp.cumsum(closes)
    gap_fwd = restarts_upto[jnp.maximum(target - 1, 0)] - restarts_upto[source]
    forward = (source < target) & (gap_fwd == 0)
    gap_bwd = closes_upto[jnp.maximum(source - 1, 0)] - closes_upto[target]
    backward = (source > target) & (gap_bwd == 0)
    return forward.astype(jnp.float32), backward.astype(jnp.float32)


def state_scan(local_state, local_norm, mask, filler):
    devices = mask.shape[0]
    heads, feats, width = local_state.shape
    norm_rows = -(-feats // width)
    room = feats - norm_rows
    norm_block = jnp.pad(local_norm, ((0, 0), (0, norm_rows * width - feats)))
    packed = lax.dynamic_update_slice(
        local_state, norm_block.reshape(heads, norm_rows, width), (0, room, 0)
    ).reshape(devices, -1, width)
    chunks = lax.all_to_all(packed, "ctx", 0, 0, tiled=True)
    chunks, filler = lax.optimization_barrier((chunks, filler))
    summed = jnp.einsum("ij,jrc->irc", mask, chunks, precision=high)
    back = lax.all_to_all(summed, "ctx", 0, 0, tiled=True).reshape(heads, feats, width)
    norm_in = back[:, room:].reshape(heads, norm_rows * width)[:, :feats]
    return (back, norm_in, filler)


def local(query, key, value_in, gate, conv_weight, doc_lengths, d_out):
    tok_rows = query.shape[0]
    channels = value_in.shape[1]
    dev_index = lax.axis_index("ctx")
    first_pos = dev_index * tok_rows
    local_pos = jnp.arange(tok_rows, dtype=jnp.int32)
    doc_ids = document_ids(doc_lengths, first_pos + local_pos)
    edge_docs = document_ids(doc_lengths, first_pos + jnp.array([-1, tok_rows], jnp.int32))
    prev_doc = edge_docs[0]
    next_doc = edge_docs[1]
    before_ids = document_ids(
        doc_lengths, first_pos - (CONV - 1) + jnp.arange(CONV - 1, dtype=jnp.int32)
    )
    after_ids = document_ids(
        doc_lengths, first_pos + tok_rows + jnp.arange(CONV - 1, dtype=jnp.int32)
    )
    taps = conv_weight.astype(jnp.float32)
    earlier = shifted(value_in[tok_rows - (CONV - 1) :], "ctx", 1)
    extended = jnp.concatenate([earlier, value_in], axis=0)
    extended_ids = jnp.concatenate([before_ids, doc_ids], axis=0)
    convolved = jnp.zeros((tok_rows, channels), jnp.float32)
    for offset in range(CONV):
        lower_row = CONV - 1 - offset
        keep = (extended_ids[lower_row : lower_row + tok_rows] == doc_ids).astype(jnp.float32)
        convolved = (
            convolved
            + taps[offset][None, :]
            * extended[lower_row : lower_row + tok_rows].astype(jnp.float32)
            * keep[:, None]
        )
    opening = jax.nn.sigmoid(gate.astype(jnp.float32))
    value_rows = (convolved * opening).astype(jnp.bfloat16)
    q_float = query.astype(jnp.float32).reshape(tok_rows, HEADS, KD)
    k_float = key.astype(jnp.float32).reshape(tok_rows, HEADS, KD)
    v_float = value_rows.astype(jnp.float32).reshape(tok_rows, HEADS, VD)
    scores = (
        jnp.einsum(
            "thd,shd->hts",
            query.reshape(tok_rows, HEADS, KD),
            key.reshape(tok_rows, HEADS, KD),
            preferred_element_type=jnp.float32,
        )
        * 0.25
    )
    kernel = 1.0 + scores + 0.5 * scores * scores
    allowed = (local_pos[:, None] >= local_pos[None, :]) & (doc_ids[:, None] == doc_ids[None, :])
    weights = jnp.where(allowed[None], kernel, 0.0)
    numerator = jnp.einsum("hts,shv->thv", weights, v_float, precision=high)
    denominator = jnp.transpose(jnp.sum(weights, axis=2), (1, 0))
    phi_query, spread_query = feature_rows(query.reshape(tok_rows, HEADS, KD))
    phi_key, spread_key = feature_rows(key.reshape(tok_rows, HEADS, KD))
    last_mask = (doc_ids == doc_ids[tok_rows - 1]).astype(jnp.float32)
    masked_key = phi_key * last_mask[None, None, :]
    local_state = jnp.einsum("hft,thv->hfv", masked_key, v_float, precision=high)
    local_norm = jnp.sum(masked_key, axis=2)
    restart_all, closes_all = block_flags(doc_lengths, lax.axis_size("ctx"), tok_rows)
    forward_mask, backward_mask = scan_masks(restart_all, closes_all)
    state_in, norm_in, (numerator, denominator) = state_scan(
        local_state, local_norm, forward_mask, (numerator, denominator)
    )
    inside = (doc_ids == prev_doc).astype(jnp.float32)
    numerator = numerator + inside[:, None, None] * jnp.einsum(
        "hft,hfv->thv", phi_query, state_in, precision=high
    )
    denominator = denominator + inside[:, None] * jnp.einsum(
        "hft,hf->th", phi_query, norm_in, precision=high
    )
    attended = numerator / denominator[:, :, None]
    mixed = attended.reshape(tok_rows, HEADS * VD).astype(jnp.bfloat16)
    upstream = d_out.astype(jnp.float32).reshape(tok_rows, HEADS, VD)
    grad_num = upstream / denominator[:, :, None]
    grad_den = -jnp.sum(upstream * attended, axis=2) / denominator
    first_mask = (doc_ids == doc_ids[0]).astype(jnp.float32)
    masked_query = phi_query * first_mask[None, None, :]
    back_state = jnp.einsum("hft,thv->hfv", masked_query, grad_num, precision=high)
    back_norm = jnp.einsum("hft,th->hf", masked_query, grad_den, precision=high)
    outside = (doc_ids == next_doc).astype(jnp.float32)
    grad_v = jnp.einsum("hts,thv->shv", weights, grad_num, precision=high)
    grad_weights = (
        jnp.einsum("thv,shv->hts", grad_num, v_float, precision=high)
        + jnp.transpose(grad_den, (1, 0))[:, :, None]
    )
    grad_scores = jnp.where(allowed[None], grad_weights * (1.0 + scores), 0.0)
    grad_q = jnp.einsum("hts,shd->thd", grad_scores, k_float, precision=high) * 0.25
    grad_k = jnp.einsum("hts,thd->shd", grad_scores, q_float, precision=high) * 0.25
    grad_phi_query = inside[None, None, :] * (
        jnp.einsum("hfv,thv->hft", state_in, grad_num, precision=high)
        + norm_in[:, :, None] * jnp.transpose(grad_den, (1, 0))[:, None, :]
    )
    grad_q = grad_q + feature_grad(grad_phi_query, spread_query)
    grad_state_in, grad_norm_in, (grad_v, grad_q, grad_k) = state_scan(
        back_state, back_norm, backward_mask, (grad_v, grad_q, grad_k)
    )
    grad_v_local = grad_v
    grad_v = grad_v + outside[:, None, None] * jnp.einsum(
        "hfs,hfv->shv", phi_key, grad_state_in, precision=high
    )
    grad_phi_key = outside[None, None, :] * (
        jnp.einsum("hfv,shv->hfs", grad_state_in, v_float, precision=high)
        + grad_norm_in[:, :, None]
    )
    grad_k = grad_k + feature_grad(grad_phi_key, spread_key)
    grad_query = grad_q.reshape(tok_rows, HEADS * KD).astype(jnp.bfloat16)
    grad_key = grad_k.reshape(tok_rows, HEADS * KD).astype(jnp.bfloat16)
    grad_core = grad_v.reshape(tok_rows, channels)
    grad_gate = (grad_core * convolved * opening * (1.0 - opening)).astype(jnp.bfloat16)
    grad_conv = grad_core * opening
    edge_grad = grad_v_local[: CONV - 1] + outside[: CONV - 1, None, None] * jnp.einsum(
        "hfs,hfv->shv", phi_key[:, :, : CONV - 1], grad_state_in, precision=high
    )
    edge_conv = edge_grad.reshape(CONV - 1, channels) * opening[: CONV - 1]
    later_rows = shifted(edge_conv, "ctx", -1)
    ahead = jnp.concatenate([grad_conv, later_rows], axis=0)
    ahead_ids = jnp.concatenate([doc_ids, after_ids], axis=0)
    grad_value = jnp.zeros((tok_rows, channels), jnp.float32)
    for offset in range(CONV):
        keep = (ahead_ids[offset : offset + tok_rows] == doc_ids).astype(jnp.float32)
        grad_value = (
            grad_value + taps[offset][None, :] * ahead[offset : offset + tok_rows] * keep[:, None]
        )
    return (mixed, grad_query, grad_key, grad_value.astype(jnp.bfloat16), grad_gate)


def solution(mesh):
    placed = (
        P(("dp", "ctx"), None),
        P(("dp", "ctx"), None),
        P(("dp", "ctx"), None),
        P(("dp", "ctx"), None),
        P(),
        P("dp"),
        P(("dp", "ctx"), None),
    )
    return jax.shard_map(
        local,
        mesh=mesh,
        in_specs=placed,
        out_specs=(
            P(("dp", "ctx"), None),
            P(("dp", "ctx"), None),
            P(("dp", "ctx"), None),
            P(("dp", "ctx"), None),
            P(("dp", "ctx"), None),
        ),
        check_vma=False,
    )
```

```python
import math

import jax
import numpy as np
import jax.numpy as jnp
from jax import lax
from jax.sharding import PartitionSpec as P

HEADS = 8
KD = 16
VD = 128
CONV = 3


highest = lax.Precision.HIGHEST
high = lax.Precision.HIGH
quad_scale = 1.0 / (4.0 * math.sqrt(2.0))


def shifted(block, axis, distance):
    devices = range(lax.axis_size(axis))
    route = [(i - distance, i) for i in devices if i - distance in devices]
    return lax.ppermute(block, axis, route)


def document_ids(lengths, positions):
    ends = jnp.cumsum(lengths, dtype=jnp.int32)
    counted = jnp.sum((ends[None, :] <= positions[:, None]).astype(jnp.int32), axis=1)
    return jnp.where(positions < 0, jnp.int32(-1), counted)


def pair_tables(width):
    rows, cols = np.triu_indices(width)
    quad_weight = np.where(rows == cols, quad_scale, quad_scale * math.sqrt(2.0))
    first = np.concatenate([[-1], np.full(width, -1), rows])
    second = np.concatenate([[-1], np.arange(width), cols])
    scale = np.concatenate([[1.0], np.full(width, 0.5), quad_weight]).astype(np.float32)
    feats = scale.size
    padded = -(-(feats + -(-feats // 128)) // 8) * 8
    extra = padded - feats
    first = np.concatenate([first, np.full(extra, width)])
    second = np.concatenate([second, np.full(extra, width)])
    scale = np.concatenate([scale, np.zeros(extra, np.float32)])
    dims = np.arange(width)
    pick_first = (first[:, None] == dims[None, :]).astype(np.float32)
    pick_second = (second[:, None] == dims[None, :]).astype(np.float32)
    return pick_first, (first < 0).astype(np.float32), pick_second, (second < 0).astype(np.float32), scale


def feature_rows(values):
    token_count, head_count, width = values.shape
    pick_first, one_first, pick_second, one_second, scale = pair_tables(width)
    picks = jnp.asarray(np.stack([pick_first, pick_second]), jnp.bfloat16)
    chosen = jnp.einsum("pfd,thd->phft", picks, values, preferred_element_type=jnp.float32)
    left = chosen[0] + jnp.asarray(one_first)[None, :, None]
    right = chosen[1] + jnp.asarray(one_second)[None, :, None]
    return (jnp.asarray(scale)[None, :, None] * left * right, (left, right))


def feature_grad(grad_phi, factors):
    left, right = factors
    width = 16
    pick_first, _, pick_second, _, scale = pair_tables(width)
    scaled = grad_phi * jnp.asarray(scale)[None, :, None]
    picks = jnp.asarray(np.concatenate([pick_first, pick_second], axis=0))
    both = jnp.concatenate([scaled * right, scaled * left], axis=1)
    return jnp.einsum("fd,hft->thd", picks, both, precision=high)


def block_flags(doc_lengths, devices, rows):
    firsts = jnp.arange(devices, dtype=jnp.int32) * rows
    prev_docs = document_ids(doc_lengths, firsts - 1)
    first_docs = document_ids(doc_lengths, firsts)
    last_docs = document_ids(doc_lengths, firsts + rows - 1)
    next_docs = document_ids(doc_lengths, firsts + rows)
    return (last_docs != prev_docs).astype(jnp.int32), (first_docs != next_docs).astype(jnp.int32)


def scan_masks(restart, closes):
    devices = restart.shape[0]
    order = jnp.arange(devices, dtype=jnp.int32)
    target = order[:, None]
    source = order[None, :]
    restarts_upto = jnp.cumsum(restart)
    closes_upto = jnp.cumsum(closes)
    gap_fwd = restarts_upto[jnp.maximum(target - 1, 0)] - restarts_upto[source]
    forward = (source < target) & (gap_fwd == 0)
    gap_bwd = closes_upto[jnp.maximum(source - 1, 0)] - closes_upto[target]
    backward = (source > target) & (gap_bwd == 0)
    return forward.astype(jnp.float32), backward.astype(jnp.float32)


def state_scan(local_state, local_norm, mask, filler, later_filler):
    devices = mask.shape[0]
    heads, feats, width = local_state.shape
    norm_rows = -(-feats // width)
    room = feats - norm_rows
    norm_block = jnp.pad(local_norm, ((0, 0), (0, norm_rows * width - feats)))
    packed = lax.dynamic_update_slice(
        local_state, norm_block.reshape(heads, norm_rows, width), (0, room, 0)
    ).reshape(devices, -1, width)
    chunks = lax.all_to_all(packed, "ctx", 0, 0, tiled=True)
    chunks, filler = lax.optimization_barrier((chunks, filler))
    summed = jnp.einsum("ij,jrc->irc", mask, chunks, precision=high)
    back = lax.all_to_all(summed, "ctx", 0, 0, tiled=True)
    back, later_filler = lax.optimization_barrier((back, later_filler))
    back = back.reshape(heads, feats, width)
    norm_in = back[:, room:].reshape(heads, norm_rows * width)[:, :feats]
    return (back, norm_in, filler, later_filler)


def local(query, key, value_in, gate, conv_weight, doc_lengths, d_out):
    tok_rows = query.shape[0]
    channels = value_in.shape[1]
    dev_index = lax.axis_index("ctx")
    first_pos = dev_index * tok_rows
    local_pos = jnp.arange(tok_rows, dtype=jnp.int32)
    doc_ids = document_ids(doc_lengths, first_pos + local_pos)
    edge_docs = document_ids(doc_lengths, first_pos + jnp.array([-1, tok_rows], jnp.int32))
    prev_doc = edge_docs[0]
    next_doc = edge_docs[1]
    before_ids = document_ids(
        doc_lengths, first_pos - (CONV - 1) + jnp.arange(CONV - 1, dtype=jnp.int32)
    )
    after_ids = document_ids(
        doc_lengths, first_pos + tok_rows + jnp.arange(CONV - 1, dtype=jnp.int32)
    )
    taps = conv_weight.astype(jnp.float32)
    earlier = shifted(value_in[tok_rows - (CONV - 1) :], "ctx", 1)
    extended = jnp.concatenate([earlier, value_in], axis=0)
    extended_ids = jnp.concatenate([before_ids, doc_ids], axis=0)
    convolved = jnp.zeros((tok_rows, channels), jnp.float32)
    for offset in range(CONV):
        lower_row = CONV - 1 - offset
        keep = (extended_ids[lower_row : lower_row + tok_rows] == doc_ids).astype(jnp.float32)
        convolved = (
            convolved
            + taps[offset][None, :]
            * extended[lower_row : lower_row + tok_rows].astype(jnp.float32)
            * keep[:, None]
        )
    opening = jax.nn.sigmoid(gate.astype(jnp.float32))
    value_rows = (convolved * opening).astype(jnp.bfloat16)
    q_float = query.astype(jnp.float32).reshape(tok_rows, HEADS, KD)
    k_float = key.astype(jnp.float32).reshape(tok_rows, HEADS, KD)
    v_float = value_rows.astype(jnp.float32).reshape(tok_rows, HEADS, VD)
    scores = (
        jnp.einsum(
            "thd,shd->hts",
            query.reshape(tok_rows, HEADS, KD),
            key.reshape(tok_rows, HEADS, KD),
            preferred_element_type=jnp.float32,
        )
        * 0.25
    )
    kernel = 1.0 + scores + 0.5 * scores * scores
    allowed = (local_pos[:, None] >= local_pos[None, :]) & (doc_ids[:, None] == doc_ids[None, :])
    weights = jnp.where(allowed[None], kernel, 0.0)
    numerator = jnp.einsum("hts,shv->thv", weights, v_float, precision=high)
    denominator = jnp.transpose(jnp.sum(weights, axis=2), (1, 0))
    phi_query, spread_query = feature_rows(query.reshape(tok_rows, HEADS, KD))
    phi_key, spread_key = feature_rows(key.reshape(tok_rows, HEADS, KD))
    last_mask = (doc_ids == doc_ids[tok_rows - 1]).astype(jnp.float32)
    masked_key = phi_key * last_mask[None, None, :]
    local_state = jnp.einsum("hft,thv->hfv", masked_key, v_float, precision=high)
    local_norm = jnp.sum(masked_key, axis=2)
    restart_all, closes_all = block_flags(doc_lengths, lax.axis_size("ctx"), tok_rows)
    forward_mask, backward_mask = scan_masks(restart_all, closes_all)
    upstream_values = jnp.einsum(
        "thv,shv->hts",
        d_out.reshape(tok_rows, HEADS, VD),
        value_rows.reshape(tok_rows, HEADS, VD),
        preferred_element_type=jnp.float32,
    )
    gate_slope = convolved * opening * (1.0 - opening)
    state_in, norm_in, (numerator, denominator), (upstream_values, gate_slope) = state_scan(
        local_state, local_norm, forward_mask, (numerator, denominator), (upstream_values, gate_slope)
    )
    inside = (doc_ids == prev_doc).astype(jnp.float32)
    numerator = numerator + inside[:, None, None] * jnp.einsum(
        "hft,hfv->thv", phi_query, state_in, precision=high
    )
    denominator = denominator + inside[:, None] * jnp.einsum(
        "hft,hf->th", phi_query, norm_in, precision=high
    )
    attended = numerator / denominator[:, :, None]
    mixed = attended.reshape(tok_rows, HEADS * VD).astype(jnp.bfloat16)
    upstream = d_out.astype(jnp.float32).reshape(tok_rows, HEADS, VD)
    grad_num = upstream / denominator[:, :, None]
    grad_den = -jnp.sum(upstream * attended, axis=2) / denominator
    first_mask = (doc_ids == doc_ids[0]).astype(jnp.float32)
    masked_query = phi_query * first_mask[None, None, :]
    back_state = jnp.einsum("hft,thv->hfv", masked_query, grad_num, precision=high)
    back_norm = jnp.einsum("hft,th->hf", masked_query, grad_den, precision=high)
    outside = (doc_ids == next_doc).astype(jnp.float32)
    grad_v = jnp.einsum("hts,thv->shv", weights, grad_num, precision=high)
    grad_weights = (
        upstream_values / jnp.transpose(denominator, (1, 0))[:, :, None]
        + jnp.transpose(grad_den, (1, 0))[:, :, None]
    )
    grad_scores = jnp.where(allowed[None], grad_weights * (1.0 + scores), 0.0)
    grad_q = jnp.einsum("hts,shd->thd", grad_scores, k_float, precision=high) * 0.25
    grad_k = jnp.einsum("hts,thd->shd", grad_scores, q_float, precision=high) * 0.25
    grad_phi_query = inside[None, None, :] * (
        jnp.einsum("hfv,thv->hft", state_in, grad_num, precision=high)
        + norm_in[:, :, None] * jnp.transpose(grad_den, (1, 0))[:, None, :]
    )
    grad_q = grad_q + feature_grad(grad_phi_query, spread_query)
    grad_state_in, grad_norm_in, (grad_v, grad_q, grad_k), _ = state_scan(
        back_state, back_norm, backward_mask, (grad_v, grad_q, grad_k), ()
    )
    grad_v = grad_v + outside[:, None, None] * jnp.einsum(
        "hfs,hfv->shv", phi_key, grad_state_in, precision=high
    )
    grad_phi_key = outside[None, None, :] * (
        jnp.einsum("hfv,shv->hfs", grad_state_in, v_float, precision=high)
        + grad_norm_in[:, :, None]
    )
    grad_k = grad_k + feature_grad(grad_phi_key, spread_key)
    grad_query = grad_q.reshape(tok_rows, HEADS * KD).astype(jnp.bfloat16)
    grad_key = grad_k.reshape(tok_rows, HEADS * KD).astype(jnp.bfloat16)
    grad_core = grad_v.reshape(tok_rows, channels)
    grad_gate = (grad_core * gate_slope).astype(jnp.bfloat16)
    grad_conv = grad_core * opening
    later_rows = shifted(grad_conv[: CONV - 1], "ctx", -1)
    ahead = jnp.concatenate([grad_conv, later_rows], axis=0)
    ahead_ids = jnp.concatenate([doc_ids, after_ids], axis=0)
    grad_value = jnp.zeros((tok_rows, channels), jnp.float32)
    for offset in range(CONV):
        keep = (ahead_ids[offset : offset + tok_rows] == doc_ids).astype(jnp.float32)
        grad_value = (
            grad_value + taps[offset][None, :] * ahead[offset : offset + tok_rows] * keep[:, None]
        )
    return (mixed, grad_query, grad_key, grad_value.astype(jnp.bfloat16), grad_gate)


def solution(mesh):
    placed = (
        P(("dp", "ctx"), None),
        P(("dp", "ctx"), None),
        P(("dp", "ctx"), None),
        P(("dp", "ctx"), None),
        P(),
        P("dp"),
        P(("dp", "ctx"), None),
    )
    return jax.shard_map(
        local,
        mesh=mesh,
        in_specs=placed,
        out_specs=(
            P(("dp", "ctx"), None),
            P(("dp", "ctx"), None),
            P(("dp", "ctx"), None),
            P(("dp", "ctx"), None),
            P(("dp", "ctx"), None),
        ),
        check_vma=False,
    )
```

```python
import math

import jax
import numpy as np
import jax.numpy as jnp
from jax import lax
from jax.sharding import PartitionSpec as P

HEADS = 8
KD = 16
VD = 128
CONV = 3


highest = lax.Precision.HIGHEST
high = lax.Precision.HIGH
quad_scale = 1.0 / (4.0 * math.sqrt(2.0))


def shifted(block, axis, distance):
    devices = range(lax.axis_size(axis))
    route = [(i - distance, i) for i in devices if i - distance in devices]
    return lax.ppermute(block, axis, route)


def document_ids(lengths, positions):
    ends = jnp.cumsum(lengths, dtype=jnp.int32)
    counted = jnp.sum((ends[None, :] <= positions[:, None]).astype(jnp.int32), axis=1)
    return jnp.where(positions < 0, jnp.int32(-1), counted)


def pair_tables(width):
    rows, cols = np.triu_indices(width)
    quad_weight = np.where(rows == cols, quad_scale, quad_scale * math.sqrt(2.0))
    first = np.concatenate([[-1], np.full(width, -1), rows])
    second = np.concatenate([[-1], np.arange(width), cols])
    scale = np.concatenate([[1.0], np.full(width, 0.5), quad_weight]).astype(np.float32)
    feats = scale.size
    padded = -(-(feats + -(-feats // 128)) // 8) * 8
    extra = padded - feats
    first = np.concatenate([first, np.full(extra, width)])
    second = np.concatenate([second, np.full(extra, width)])
    scale = np.concatenate([scale, np.zeros(extra, np.float32)])
    dims = np.arange(width)
    pick_first = (first[:, None] == dims[None, :]).astype(np.float32)
    pick_second = (second[:, None] == dims[None, :]).astype(np.float32)
    return pick_first, (first < 0).astype(np.float32), pick_second, (second < 0).astype(np.float32), scale


def feature_rows(values):
    token_count, head_count, width = values.shape
    pick_first, one_first, pick_second, one_second, scale = pair_tables(width)
    picks = jnp.asarray(np.stack([pick_first, pick_second]), jnp.bfloat16)
    chosen = jnp.einsum("pfd,thd->phft", picks, values, preferred_element_type=jnp.float32)
    left = chosen[0] + jnp.asarray(one_first)[None, :, None]
    right = chosen[1] + jnp.asarray(one_second)[None, :, None]
    return (jnp.asarray(scale)[None, :, None] * left * right, (left, right))


def feature_grad(grad_phi, factors):
    left, right = factors
    width = 16
    pick_first, _, pick_second, _, scale = pair_tables(width)
    scaled = grad_phi * jnp.asarray(scale)[None, :, None]
    picks = jnp.asarray(np.concatenate([pick_first, pick_second], axis=0))
    both = jnp.concatenate([scaled * right, scaled * left], axis=1)
    return jnp.einsum("fd,hft->thd", picks, both, precision=high)


def block_flags(doc_lengths, devices, rows):
    firsts = jnp.arange(devices, dtype=jnp.int32) * rows
    prev_docs = document_ids(doc_lengths, firsts - 1)
    first_docs = document_ids(doc_lengths, firsts)
    last_docs = document_ids(doc_lengths, firsts + rows - 1)
    next_docs = document_ids(doc_lengths, firsts + rows)
    return (last_docs != prev_docs).astype(jnp.int32), (first_docs != next_docs).astype(jnp.int32)


def scan_masks(restart, closes):
    devices = restart.shape[0]
    order = jnp.arange(devices, dtype=jnp.int32)
    target = order[:, None]
    source = order[None, :]
    restarts_upto = jnp.cumsum(restart)
    closes_upto = jnp.cumsum(closes)
    gap_fwd = restarts_upto[jnp.maximum(target - 1, 0)] - restarts_upto[source]
    forward = (source < target) & (gap_fwd == 0)
    gap_bwd = closes_upto[jnp.maximum(source - 1, 0)] - closes_upto[target]
    backward = (source > target) & (gap_bwd == 0)
    return forward.astype(jnp.float32), backward.astype(jnp.float32)


def state_scan(local_state, local_norm, mask, filler, later_filler):
    devices = mask.shape[0]
    heads, feats, width = local_state.shape
    norm_rows = -(-feats // width)
    room = feats - norm_rows
    norm_block = jnp.pad(local_norm, ((0, 0), (0, norm_rows * width - feats)))
    packed = lax.dynamic_update_slice(
        local_state, norm_block.reshape(heads, norm_rows, width), (0, room, 0)
    ).reshape(devices, -1, width)
    chunks = lax.all_to_all(packed, "ctx", 0, 0, tiled=True)
    chunks, filler = lax.optimization_barrier((chunks, filler))
    summed = jnp.einsum("ij,jrc->irc", mask, chunks, precision=high)
    back = lax.all_to_all(summed, "ctx", 0, 0, tiled=True)
    back, later_filler = lax.optimization_barrier((back, later_filler))
    back = back.reshape(heads, feats, width)
    norm_in = back[:, room:].reshape(heads, norm_rows * width)[:, :feats]
    return (back, norm_in, filler, later_filler)


def local(query, key, value_in, gate, conv_weight, doc_lengths, d_out):
    tok_rows = query.shape[0]
    channels = value_in.shape[1]
    dev_index = lax.axis_index("ctx")
    first_pos = dev_index * tok_rows
    local_pos = jnp.arange(tok_rows, dtype=jnp.int32)
    doc_ids = document_ids(doc_lengths, first_pos + local_pos)
    edge_docs = document_ids(doc_lengths, first_pos + jnp.array([-1, tok_rows], jnp.int32))
    prev_doc = edge_docs[0]
    next_doc = edge_docs[1]
    before_ids = document_ids(
        doc_lengths, first_pos - (CONV - 1) + jnp.arange(CONV - 1, dtype=jnp.int32)
    )
    after_ids = document_ids(
        doc_lengths, first_pos + tok_rows + jnp.arange(CONV - 1, dtype=jnp.int32)
    )
    taps = conv_weight.astype(jnp.float32)
    earlier = shifted(value_in[tok_rows - (CONV - 1) :], "ctx", 1)
    extended = jnp.concatenate([earlier, value_in], axis=0)
    extended_ids = jnp.concatenate([before_ids, doc_ids], axis=0)
    convolved = jnp.zeros((tok_rows, channels), jnp.float32)
    for offset in range(CONV):
        lower_row = CONV - 1 - offset
        keep = (extended_ids[lower_row : lower_row + tok_rows] == doc_ids).astype(jnp.float32)
        convolved = (
            convolved
            + taps[offset][None, :]
            * extended[lower_row : lower_row + tok_rows].astype(jnp.float32)
            * keep[:, None]
        )
    opening = jax.nn.sigmoid(gate.astype(jnp.float32))
    value_rows = (convolved * opening).astype(jnp.bfloat16)
    q_float = query.astype(jnp.float32).reshape(tok_rows, HEADS, KD)
    k_float = key.astype(jnp.float32).reshape(tok_rows, HEADS, KD)
    v_float = value_rows.astype(jnp.float32).reshape(tok_rows, HEADS, VD)
    scores = (
        jnp.einsum(
            "thd,shd->hts",
            query.reshape(tok_rows, HEADS, KD),
            key.reshape(tok_rows, HEADS, KD),
            preferred_element_type=jnp.float32,
        )
        * 0.25
    )
    kernel = 1.0 + scores + 0.5 * scores * scores
    allowed = (local_pos[:, None] >= local_pos[None, :]) & (doc_ids[:, None] == doc_ids[None, :])
    weights = jnp.where(allowed[None], kernel, 0.0)
    numerator = jnp.einsum("hts,shv->thv", weights, v_float, precision=high)
    denominator = jnp.transpose(jnp.sum(weights, axis=2), (1, 0))
    phi_query, spread_query = feature_rows(query.reshape(tok_rows, HEADS, KD))
    phi_key, spread_key = feature_rows(key.reshape(tok_rows, HEADS, KD))
    last_mask = (doc_ids == doc_ids[tok_rows - 1]).astype(jnp.float32)
    masked_key = phi_key * last_mask[None, None, :]
    local_state = jnp.einsum("hft,thv->hfv", masked_key, v_float, precision=high)
    local_norm = jnp.sum(masked_key, axis=2)
    restart_all, closes_all = block_flags(doc_lengths, lax.axis_size("ctx"), tok_rows)
    forward_mask, backward_mask = scan_masks(restart_all, closes_all)
    gate_slope = convolved * opening * (1.0 - opening)
    state_in, norm_in, (numerator, denominator), gate_slope = state_scan(
        local_state, local_norm, forward_mask, (numerator, denominator), gate_slope
    )
    inside = (doc_ids == prev_doc).astype(jnp.float32)
    numerator = numerator + inside[:, None, None] * jnp.einsum(
        "hft,hfv->thv", phi_query, state_in, precision=high
    )
    denominator = denominator + inside[:, None] * jnp.einsum(
        "hft,hf->th", phi_query, norm_in, precision=high
    )
    attended = numerator / denominator[:, :, None]
    mixed = attended.reshape(tok_rows, HEADS * VD).astype(jnp.bfloat16)
    upstream = d_out.astype(jnp.float32).reshape(tok_rows, HEADS, VD)
    grad_num = upstream / denominator[:, :, None]
    grad_den = -jnp.sum(upstream * attended, axis=2) / denominator
    first_mask = (doc_ids == doc_ids[0]).astype(jnp.float32)
    masked_query = phi_query * first_mask[None, None, :]
    back_state = jnp.einsum("hft,thv->hfv", masked_query, grad_num, precision=high)
    back_norm = jnp.einsum("hft,th->hf", masked_query, grad_den, precision=high)
    outside = (doc_ids == next_doc).astype(jnp.float32)
    grad_v = jnp.einsum("hts,thv->shv", weights, grad_num, precision=high)
    grad_weights = (
        jnp.einsum("thv,shv->hts", grad_num, v_float, precision=high)
        + jnp.transpose(grad_den, (1, 0))[:, :, None]
    )
    grad_scores = jnp.where(allowed[None], grad_weights * (1.0 + scores), 0.0)
    grad_q = jnp.einsum("hts,shd->thd", grad_scores, k_float, precision=high) * 0.25
    grad_k = jnp.einsum("hts,thd->shd", grad_scores, q_float, precision=high) * 0.25
    grad_phi_query = inside[None, None, :] * (
        jnp.einsum("hfv,thv->hft", state_in, grad_num, precision=high)
        + norm_in[:, :, None] * jnp.transpose(grad_den, (1, 0))[:, None, :]
    )
    grad_q = grad_q + feature_grad(grad_phi_query, spread_query)
    grad_state_in, grad_norm_in, (grad_v, grad_q, grad_k), _ = state_scan(
        back_state, back_norm, backward_mask, (grad_v, grad_q, grad_k), ()
    )
    grad_v = grad_v + outside[:, None, None] * jnp.einsum(
        "hfs,hfv->shv", phi_key, grad_state_in, precision=high
    )
    grad_phi_key = outside[None, None, :] * (
        jnp.einsum("hfv,shv->hfs", grad_state_in, v_float, precision=high)
        + grad_norm_in[:, :, None]
    )
    grad_k = grad_k + feature_grad(grad_phi_key, spread_key)
    grad_query = grad_q.reshape(tok_rows, HEADS * KD).astype(jnp.bfloat16)
    grad_key = grad_k.reshape(tok_rows, HEADS * KD).astype(jnp.bfloat16)
    grad_core = grad_v.reshape(tok_rows, channels)
    grad_gate = (grad_core * gate_slope).astype(jnp.bfloat16)
    grad_conv = grad_core * opening
    later_rows = shifted(grad_conv[: CONV - 1], "ctx", -1)
    ahead = jnp.concatenate([grad_conv, later_rows], axis=0)
    ahead_ids = jnp.concatenate([doc_ids, after_ids], axis=0)
    grad_value = jnp.zeros((tok_rows, channels), jnp.float32)
    for offset in range(CONV):
        keep = (ahead_ids[offset : offset + tok_rows] == doc_ids).astype(jnp.float32)
        grad_value = (
            grad_value + taps[offset][None, :] * ahead[offset : offset + tok_rows] * keep[:, None]
        )
    return (mixed, grad_query, grad_key, grad_value.astype(jnp.bfloat16), grad_gate)


def solution(mesh):
    placed = (
        P(("dp", "ctx"), None),
        P(("dp", "ctx"), None),
        P(("dp", "ctx"), None),
        P(("dp", "ctx"), None),
        P(),
        P("dp"),
        P(("dp", "ctx"), None),
    )
    return jax.shard_map(
        local,
        mesh=mesh,
        in_specs=placed,
        out_specs=(
            P(("dp", "ctx"), None),
            P(("dp", "ctx"), None),
            P(("dp", "ctx"), None),
            P(("dp", "ctx"), None),
            P(("dp", "ctx"), None),
        ),
        check_vma=False,
    )
```

```python
import math

import jax
import numpy as np
import jax.numpy as jnp
from jax import lax
from jax.sharding import PartitionSpec as P

HEADS = 8
KD = 16
VD = 128
CONV = 3


highest = lax.Precision.HIGHEST
high = lax.Precision.HIGH
quad_scale = 1.0 / (4.0 * math.sqrt(2.0))


def shifted(block, axis, distance):
    devices = range(lax.axis_size(axis))
    route = [(i - distance, i) for i in devices if i - distance in devices]
    return lax.ppermute(block, axis, route)


def document_ids(lengths, positions):
    ends = jnp.cumsum(lengths, dtype=jnp.int32)
    counted = jnp.sum((ends[None, :] <= positions[:, None]).astype(jnp.int32), axis=1)
    return jnp.where(positions < 0, jnp.int32(-1), counted)


def pair_tables(width):
    rows, cols = np.triu_indices(width)
    quad_weight = np.where(rows == cols, quad_scale, quad_scale * math.sqrt(2.0))
    first = np.concatenate([[-1], np.full(width, -1), rows])
    second = np.concatenate([[-1], np.arange(width), cols])
    scale = np.concatenate([[1.0], np.full(width, 0.5), quad_weight]).astype(np.float32)
    feats = scale.size
    padded = -(-(feats + -(-feats // 128)) // 8) * 8
    extra = padded - feats
    first = np.concatenate([first, np.full(extra, width)])
    second = np.concatenate([second, np.full(extra, width)])
    scale = np.concatenate([scale, np.zeros(extra, np.float32)])
    dims = np.arange(width)
    pick_first = (first[:, None] == dims[None, :]).astype(np.float32)
    pick_second = (second[:, None] == dims[None, :]).astype(np.float32)
    return pick_first, (first < 0).astype(np.float32), pick_second, (second < 0).astype(np.float32), scale


def feature_rows(values):
    token_count, head_count, width = values.shape
    pick_first, one_first, pick_second, one_second, scale = pair_tables(width)
    picks = jnp.asarray(np.stack([pick_first, pick_second]), jnp.bfloat16)
    chosen = jnp.einsum("pfd,thd->phft", picks, values, preferred_element_type=jnp.float32)
    left = chosen[0] + jnp.asarray(one_first)[None, :, None]
    right = chosen[1] + jnp.asarray(one_second)[None, :, None]
    return (jnp.asarray(scale)[None, :, None] * left * right, (left, right))


def feature_grad(grad_phi, factors):
    left, right = factors
    width = 16
    pick_first, _, pick_second, _, scale = pair_tables(width)
    scaled = grad_phi * jnp.asarray(scale)[None, :, None]
    picks = jnp.asarray(np.concatenate([pick_first, pick_second], axis=0))
    both = jnp.concatenate([scaled * right, scaled * left], axis=1)
    return jnp.einsum("fd,hft->thd", picks, both, precision=high)


def block_flags(doc_lengths, devices, rows):
    firsts = jnp.arange(devices, dtype=jnp.int32) * rows
    prev_docs = document_ids(doc_lengths, firsts - 1)
    first_docs = document_ids(doc_lengths, firsts)
    last_docs = document_ids(doc_lengths, firsts + rows - 1)
    next_docs = document_ids(doc_lengths, firsts + rows)
    return (last_docs != prev_docs).astype(jnp.int32), (first_docs != next_docs).astype(jnp.int32)


def scan_masks(restart, closes):
    devices = restart.shape[0]
    order = jnp.arange(devices, dtype=jnp.int32)
    target = order[:, None]
    source = order[None, :]
    restarts_upto = jnp.cumsum(restart)
    closes_upto = jnp.cumsum(closes)
    gap_fwd = restarts_upto[jnp.maximum(target - 1, 0)] - restarts_upto[source]
    forward = (source < target) & (gap_fwd == 0)
    gap_bwd = closes_upto[jnp.maximum(source - 1, 0)] - closes_upto[target]
    backward = (source > target) & (gap_bwd == 0)
    return forward.astype(jnp.float32), backward.astype(jnp.float32)


def state_scan(local_state, local_norm, mask, filler):
    devices = mask.shape[0]
    heads, feats, width = local_state.shape
    norm_rows = -(-feats // width)
    room = feats - norm_rows
    norm_block = jnp.pad(local_norm, ((0, 0), (0, norm_rows * width - feats)))
    packed = lax.dynamic_update_slice(
        local_state, norm_block.reshape(heads, norm_rows, width), (0, room, 0)
    ).reshape(devices, -1, width)
    chunks = lax.all_to_all(packed, "ctx", 0, 0, tiled=True)
    chunks, filler = lax.optimization_barrier((chunks, filler))
    summed = jnp.einsum("ij,jrc->irc", mask, chunks, precision=high)
    back = lax.all_to_all(summed, "ctx", 0, 0, tiled=True).reshape(heads, feats, width)
    norm_in = back[:, room:].reshape(heads, norm_rows * width)[:, :feats]
    return (back, norm_in, filler)


def local(query, key, value_in, gate, conv_weight, doc_lengths, d_out):
    tok_rows = query.shape[0]
    channels = value_in.shape[1]
    dev_index = lax.axis_index("ctx")
    first_pos = dev_index * tok_rows
    local_pos = jnp.arange(tok_rows, dtype=jnp.int32)
    doc_ids = document_ids(doc_lengths, first_pos + local_pos)
    edge_docs = document_ids(doc_lengths, first_pos + jnp.array([-1, tok_rows], jnp.int32))
    prev_doc = edge_docs[0]
    next_doc = edge_docs[1]
    before_ids = document_ids(
        doc_lengths, first_pos - (CONV - 1) + jnp.arange(CONV - 1, dtype=jnp.int32)
    )
    after_ids = document_ids(
        doc_lengths, first_pos + tok_rows + jnp.arange(CONV - 1, dtype=jnp.int32)
    )
    taps = conv_weight.astype(jnp.float32)
    earlier = shifted(value_in[tok_rows - (CONV - 1) :], "ctx", 1)
    extended = jnp.concatenate([earlier, value_in], axis=0)
    extended_ids = jnp.concatenate([before_ids, doc_ids], axis=0)
    convolved = jnp.zeros((tok_rows, channels), jnp.float32)
    for offset in range(CONV):
        lower_row = CONV - 1 - offset
        keep = (extended_ids[lower_row : lower_row + tok_rows] == doc_ids).astype(jnp.float32)
        convolved = (
            convolved
            + taps[offset][None, :]
            * extended[lower_row : lower_row + tok_rows].astype(jnp.float32)
            * keep[:, None]
        )
    opening = jax.nn.sigmoid(gate.astype(jnp.float32))
    value_rows = (convolved * opening).astype(jnp.bfloat16)
    q_float = query.astype(jnp.float32).reshape(tok_rows, HEADS, KD)
    k_float = key.astype(jnp.float32).reshape(tok_rows, HEADS, KD)
    v_float = value_rows.astype(jnp.float32).reshape(tok_rows, HEADS, VD)
    scores = (
        jnp.einsum(
            "thd,shd->hts",
            query.reshape(tok_rows, HEADS, KD),
            key.reshape(tok_rows, HEADS, KD),
            preferred_element_type=jnp.float32,
        )
        * 0.25
    )
    kernel = 1.0 + scores + 0.5 * scores * scores
    allowed = (local_pos[:, None] >= local_pos[None, :]) & (doc_ids[:, None] == doc_ids[None, :])
    weights = jnp.where(allowed[None], kernel, 0.0)
    numerator = jnp.einsum("hts,shv->thv", weights, v_float, precision=high)
    denominator = jnp.transpose(jnp.sum(weights, axis=2), (1, 0))
    phi_query, spread_query = feature_rows(query.reshape(tok_rows, HEADS, KD))
    phi_key, spread_key = feature_rows(key.reshape(tok_rows, HEADS, KD))
    last_mask = (doc_ids == doc_ids[tok_rows - 1]).astype(jnp.float32)
    masked_key = phi_key * last_mask[None, None, :]
    local_state = jnp.einsum("hft,thv->hfv", masked_key, v_float, precision=high)
    local_norm = jnp.sum(masked_key, axis=2)
    restart_all, closes_all = block_flags(doc_lengths, lax.axis_size("ctx"), tok_rows)
    forward_mask, backward_mask = scan_masks(restart_all, closes_all)
    state_in, norm_in, _ = state_scan(local_state, local_norm, forward_mask, ())
    inside = (doc_ids == prev_doc).astype(jnp.float32)
    numerator = numerator + inside[:, None, None] * jnp.einsum(
        "hft,hfv->thv", phi_query, state_in, precision=high
    )
    denominator = denominator + inside[:, None] * jnp.einsum(
        "hft,hf->th", phi_query, norm_in, precision=high
    )
    attended = numerator / denominator[:, :, None]
    mixed = attended.reshape(tok_rows, HEADS * VD).astype(jnp.bfloat16)
    upstream = d_out.astype(jnp.float32).reshape(tok_rows, HEADS, VD)
    grad_num = upstream / denominator[:, :, None]
    grad_den = -jnp.sum(upstream * attended, axis=2) / denominator
    first_mask = (doc_ids == doc_ids[0]).astype(jnp.float32)
    masked_query = phi_query * first_mask[None, None, :]
    back_state = jnp.einsum("hft,thv->hfv", masked_query, grad_num, precision=high)
    back_norm = jnp.einsum("hft,th->hf", masked_query, grad_den, precision=high)
    outside = (doc_ids == next_doc).astype(jnp.float32)
    grad_v = jnp.einsum("hts,thv->shv", weights, grad_num, precision=high)
    grad_weights = (
        jnp.einsum("thv,shv->hts", grad_num, v_float, precision=high)
        + jnp.transpose(grad_den, (1, 0))[:, :, None]
    )
    grad_scores = jnp.where(allowed[None], grad_weights * (1.0 + scores), 0.0)
    grad_q = jnp.einsum("hts,shd->thd", grad_scores, k_float, precision=high) * 0.25
    grad_k = jnp.einsum("hts,thd->shd", grad_scores, q_float, precision=high) * 0.25
    grad_phi_query = inside[None, None, :] * (
        jnp.einsum("hfv,thv->hft", state_in, grad_num, precision=high)
        + norm_in[:, :, None] * jnp.transpose(grad_den, (1, 0))[:, None, :]
    )
    grad_q = grad_q + feature_grad(grad_phi_query, spread_query)
    grad_state_in, grad_norm_in, (grad_v, grad_q, grad_k) = state_scan(
        back_state, back_norm, backward_mask, (grad_v, grad_q, grad_k)
    )
    grad_v = grad_v + outside[:, None, None] * jnp.einsum(
        "hfs,hfv->shv", phi_key, grad_state_in, precision=high
    )
    grad_phi_key = outside[None, None, :] * (
        jnp.einsum("hfv,shv->hfs", grad_state_in, v_float, precision=high)
        + grad_norm_in[:, :, None]
    )
    grad_k = grad_k + feature_grad(grad_phi_key, spread_key)
    grad_query = grad_q.reshape(tok_rows, HEADS * KD).astype(jnp.bfloat16)
    grad_key = grad_k.reshape(tok_rows, HEADS * KD).astype(jnp.bfloat16)
    grad_core = grad_v.reshape(tok_rows, channels)
    grad_gate = (grad_core * convolved * opening * (1.0 - opening)).astype(jnp.bfloat16)
    grad_conv = grad_core * opening
    later_rows = shifted(grad_conv[: CONV - 1], "ctx", -1)
    ahead = jnp.concatenate([grad_conv, later_rows], axis=0)
    ahead_ids = jnp.concatenate([doc_ids, after_ids], axis=0)
    grad_value = jnp.zeros((tok_rows, channels), jnp.float32)
    for offset in range(CONV):
        keep = (ahead_ids[offset : offset + tok_rows] == doc_ids).astype(jnp.float32)
        grad_value = (
            grad_value + taps[offset][None, :] * ahead[offset : offset + tok_rows] * keep[:, None]
        )
    return (mixed, grad_query, grad_key, grad_value.astype(jnp.bfloat16), grad_gate)


def solution(mesh):
    placed = (
        P(("dp", "ctx"), None),
        P(("dp", "ctx"), None),
        P(("dp", "ctx"), None),
        P(("dp", "ctx"), None),
        P(),
        P("dp"),
        P(("dp", "ctx"), None),
    )
    return jax.shard_map(
        local,
        mesh=mesh,
        in_specs=placed,
        out_specs=(
            P(("dp", "ctx"), None),
            P(("dp", "ctx"), None),
            P(("dp", "ctx"), None),
            P(("dp", "ctx"), None),
            P(("dp", "ctx"), None),
        ),
        check_vma=False,
    )
```

```python
import math

import jax
import numpy as np
import jax.numpy as jnp
from jax import lax
from jax.sharding import PartitionSpec as P

HEADS = 8
KD = 16
VD = 128
CONV = 3


highest = lax.Precision.HIGHEST
high = lax.Precision.HIGH
quad_scale = 1.0 / (4.0 * math.sqrt(2.0))


def shifted(block, axis, distance):
    devices = range(lax.axis_size(axis))
    route = [(i - distance, i) for i in devices if i - distance in devices]
    return lax.ppermute(block, axis, route)


def document_ids(lengths, positions):
    ends = jnp.cumsum(lengths, dtype=jnp.int32)
    counted = jnp.sum((ends[None, :] <= positions[:, None]).astype(jnp.int32), axis=1)
    return jnp.where(positions < 0, jnp.int32(-1), counted)


def pair_tables(width):
    rows, cols = np.triu_indices(width)
    quad_weight = np.where(rows == cols, quad_scale, quad_scale * math.sqrt(2.0))
    first = np.concatenate([[-1], np.full(width, -1), rows])
    second = np.concatenate([[-1], np.arange(width), cols])
    scale = np.concatenate([[1.0], np.full(width, 0.5), quad_weight]).astype(np.float32)
    feats = scale.size
    padded = -(-(feats + -(-feats // 128)) // 8) * 8
    extra = padded - feats
    first = np.concatenate([first, np.full(extra, width)])
    second = np.concatenate([second, np.full(extra, width)])
    scale = np.concatenate([scale, np.zeros(extra, np.float32)])
    dims = np.arange(width)
    pick_first = (first[:, None] == dims[None, :]).astype(np.float32)
    pick_second = (second[:, None] == dims[None, :]).astype(np.float32)
    return pick_first, (first < 0).astype(np.float32), pick_second, (second < 0).astype(np.float32), scale


def feature_rows(values):
    token_count, head_count, width = values.shape
    pick_first, one_first, pick_second, one_second, scale = pair_tables(width)
    picks = jnp.asarray(np.stack([pick_first, pick_second]), jnp.bfloat16)
    chosen = jnp.einsum("pfd,thd->phft", picks, values, preferred_element_type=jnp.float32)
    left = chosen[0] + jnp.asarray(one_first)[None, :, None]
    right = chosen[1] + jnp.asarray(one_second)[None, :, None]
    return (jnp.asarray(scale)[None, :, None] * left * right, (left, right))


def feature_grad(grad_phi, factors):
    left, right = factors
    width = 16
    pick_first, _, pick_second, _, scale = pair_tables(width)
    scaled = grad_phi * jnp.asarray(scale)[None, :, None]
    picks = jnp.asarray(np.concatenate([pick_first, pick_second], axis=0))
    both = jnp.concatenate([scaled * right, scaled * left], axis=1)
    return jnp.einsum("fd,hft->thd", picks, both, precision=high)


def block_flags(doc_lengths, devices, rows):
    firsts = jnp.arange(devices, dtype=jnp.int32) * rows
    prev_docs = document_ids(doc_lengths, firsts - 1)
    first_docs = document_ids(doc_lengths, firsts)
    last_docs = document_ids(doc_lengths, firsts + rows - 1)
    next_docs = document_ids(doc_lengths, firsts + rows)
    return (last_docs != prev_docs).astype(jnp.int32), (first_docs != next_docs).astype(jnp.int32)


def scan_masks(restart, closes):
    devices = restart.shape[0]
    order = jnp.arange(devices, dtype=jnp.int32)
    target = order[:, None]
    source = order[None, :]
    restarts_upto = jnp.cumsum(restart)
    closes_upto = jnp.cumsum(closes)
    gap_fwd = restarts_upto[jnp.maximum(target - 1, 0)] - restarts_upto[source]
    forward = (source < target) & (gap_fwd == 0)
    gap_bwd = closes_upto[jnp.maximum(source - 1, 0)] - closes_upto[target]
    backward = (source > target) & (gap_bwd == 0)
    return forward.astype(jnp.float32), backward.astype(jnp.float32)


def state_scan(local_state, local_norm, mask, filler):
    devices = mask.shape[0]
    heads, feats, width = local_state.shape
    norm_rows = -(-feats // width)
    room = feats - norm_rows
    norm_block = jnp.pad(local_norm, ((0, 0), (0, norm_rows * width - feats)))
    packed = lax.dynamic_update_slice(
        local_state, norm_block.reshape(heads, norm_rows, width), (0, room, 0)
    ).reshape(devices, -1, width)
    chunks = lax.all_to_all(packed, "ctx", 0, 0, tiled=True)
    chunks, filler = lax.optimization_barrier((chunks, filler))
    summed = jnp.einsum("ij,jrc->irc", mask, chunks, precision=high)
    back = lax.all_to_all(summed, "ctx", 0, 0, tiled=True).reshape(heads, feats, width)
    norm_in = back[:, room:].reshape(heads, norm_rows * width)[:, :feats]
    return (back, norm_in, filler)


def local(query, key, value_in, gate, conv_weight, doc_lengths, d_out):
    tok_rows = query.shape[0]
    channels = value_in.shape[1]
    dev_index = lax.axis_index("ctx")
    first_pos = dev_index * tok_rows
    local_pos = jnp.arange(tok_rows, dtype=jnp.int32)
    doc_ids = document_ids(doc_lengths, first_pos + local_pos)
    edge_docs = document_ids(doc_lengths, first_pos + jnp.array([-1, tok_rows], jnp.int32))
    prev_doc = edge_docs[0]
    next_doc = edge_docs[1]
    before_ids = document_ids(
        doc_lengths, first_pos - (CONV - 1) + jnp.arange(CONV - 1, dtype=jnp.int32)
    )
    after_ids = document_ids(
        doc_lengths, first_pos + tok_rows + jnp.arange(CONV - 1, dtype=jnp.int32)
    )
    taps = conv_weight.astype(jnp.float32)
    earlier = shifted(value_in[tok_rows - (CONV - 1) :], "ctx", 1)
    extended = jnp.concatenate([earlier, value_in], axis=0)
    extended_ids = jnp.concatenate([before_ids, doc_ids], axis=0)
    convolved = jnp.zeros((tok_rows, channels), jnp.float32)
    for offset in range(CONV):
        lower_row = CONV - 1 - offset
        keep = (extended_ids[lower_row : lower_row + tok_rows] == doc_ids).astype(jnp.float32)
        convolved = (
            convolved
            + taps[offset][None, :]
            * extended[lower_row : lower_row + tok_rows].astype(jnp.float32)
            * keep[:, None]
        )
    opening = jax.nn.sigmoid(gate.astype(jnp.float32))
    value_rows = (convolved * opening).astype(jnp.bfloat16)
    q_float = query.astype(jnp.float32).reshape(tok_rows, HEADS, KD)
    k_float = key.astype(jnp.float32).reshape(tok_rows, HEADS, KD)
    v_float = value_rows.astype(jnp.float32).reshape(tok_rows, HEADS, VD)
    scores = (
        jnp.einsum(
            "thd,shd->hts",
            query.reshape(tok_rows, HEADS, KD),
            key.reshape(tok_rows, HEADS, KD),
            preferred_element_type=jnp.float32,
        )
        * 0.25
    )
    kernel = 1.0 + scores + 0.5 * scores * scores
    allowed = (local_pos[:, None] >= local_pos[None, :]) & (doc_ids[:, None] == doc_ids[None, :])
    weights = jnp.where(allowed[None], kernel, 0.0)
    numerator = jnp.einsum("hts,shv->thv", weights, v_float, precision=high)
    denominator = jnp.transpose(jnp.sum(weights, axis=2), (1, 0))
    phi_query, spread_query = feature_rows(query.reshape(tok_rows, HEADS, KD))
    phi_key, spread_key = feature_rows(key.reshape(tok_rows, HEADS, KD))
    last_mask = (doc_ids == doc_ids[tok_rows - 1]).astype(jnp.float32)
    masked_key = phi_key * last_mask[None, None, :]
    local_state = jnp.einsum("hft,thv->hfv", masked_key, v_float, precision=high)
    local_norm = jnp.sum(masked_key, axis=2)
    restart_all, closes_all = block_flags(doc_lengths, lax.axis_size("ctx"), tok_rows)
    forward_mask, backward_mask = scan_masks(restart_all, closes_all)
    state_in, norm_in, _ = state_scan(local_state, local_norm, forward_mask, ())
    inside = (doc_ids == prev_doc).astype(jnp.float32)
    numerator = numerator + inside[:, None, None] * jnp.einsum(
        "hft,hfv->thv", phi_query, state_in, precision=high
    )
    denominator = denominator + inside[:, None] * jnp.einsum(
        "hft,hf->th", phi_query, norm_in, precision=high
    )
    attended = numerator / denominator[:, :, None]
    mixed = attended.reshape(tok_rows, HEADS * VD).astype(jnp.bfloat16)
    upstream = d_out.astype(jnp.float32).reshape(tok_rows, HEADS, VD)
    grad_num = upstream / denominator[:, :, None]
    grad_den = -jnp.sum(upstream * attended, axis=2) / denominator
    first_mask = (doc_ids == doc_ids[0]).astype(jnp.float32)
    masked_query = phi_query * first_mask[None, None, :]
    back_state = jnp.einsum("hft,thv->hfv", masked_query, grad_num, precision=high)
    back_norm = jnp.einsum("hft,th->hf", masked_query, grad_den, precision=high)
    outside = (doc_ids == next_doc).astype(jnp.float32)
    grad_v = jnp.einsum("hts,thv->shv", weights, grad_num, precision=high)
    grad_weights = (
        jnp.einsum("thv,shv->hts", grad_num, v_float, precision=high)
        + jnp.transpose(grad_den, (1, 0))[:, :, None]
    )
    grad_scores = jnp.where(allowed[None], grad_weights * (1.0 + scores), 0.0)
    grad_q = jnp.einsum("hts,shd->thd", grad_scores, k_float, precision=high) * 0.25
    grad_k = jnp.einsum("hts,thd->shd", grad_scores, q_float, precision=high) * 0.25
    grad_phi_query = inside[None, None, :] * (
        jnp.einsum("hfv,thv->hft", state_in, grad_num, precision=high)
        + norm_in[:, :, None] * jnp.transpose(grad_den, (1, 0))[:, None, :]
    )
    grad_q = grad_q + feature_grad(grad_phi_query, spread_query)
    gate_slope = convolved * opening * (1.0 - opening)
    grad_state_in, grad_norm_in, (grad_v, grad_q, grad_k, gate_slope) = state_scan(
        back_state, back_norm, backward_mask, (grad_v, grad_q, grad_k, gate_slope)
    )
    grad_v = grad_v + outside[:, None, None] * jnp.einsum(
        "hfs,hfv->shv", phi_key, grad_state_in, precision=high
    )
    grad_phi_key = outside[None, None, :] * (
        jnp.einsum("hfv,shv->hfs", grad_state_in, v_float, precision=high)
        + grad_norm_in[:, :, None]
    )
    grad_k = grad_k + feature_grad(grad_phi_key, spread_key)
    grad_query = grad_q.reshape(tok_rows, HEADS * KD).astype(jnp.bfloat16)
    grad_key = grad_k.reshape(tok_rows, HEADS * KD).astype(jnp.bfloat16)
    grad_core = grad_v.reshape(tok_rows, channels)
    grad_gate = (grad_core * gate_slope).astype(jnp.bfloat16)
    grad_conv = grad_core * opening
    later_rows = shifted(grad_conv[: CONV - 1], "ctx", -1)
    ahead = jnp.concatenate([grad_conv, later_rows], axis=0)
    ahead_ids = jnp.concatenate([doc_ids, after_ids], axis=0)
    grad_value = jnp.zeros((tok_rows, channels), jnp.float32)
    for offset in range(CONV):
        keep = (ahead_ids[offset : offset + tok_rows] == doc_ids).astype(jnp.float32)
        grad_value = (
            grad_value + taps[offset][None, :] * ahead[offset : offset + tok_rows] * keep[:, None]
        )
    return (mixed, grad_query, grad_key, grad_value.astype(jnp.bfloat16), grad_gate)


def solution(mesh):
    placed = (
        P(("dp", "ctx"), None),
        P(("dp", "ctx"), None),
        P(("dp", "ctx"), None),
        P(("dp", "ctx"), None),
        P(),
        P("dp"),
        P(("dp", "ctx"), None),
    )
    return jax.shard_map(
        local,
        mesh=mesh,
        in_specs=placed,
        out_specs=(
            P(("dp", "ctx"), None),
            P(("dp", "ctx"), None),
            P(("dp", "ctx"), None),
            P(("dp", "ctx"), None),
            P(("dp", "ctx"), None),
        ),
        check_vma=False,
    )
```

```python
import math

import jax
import numpy as np
import jax.numpy as jnp
from jax import lax
from jax.sharding import PartitionSpec as P

HEADS = 8
KD = 16
VD = 128
CONV = 3


highest = lax.Precision.HIGHEST
high = lax.Precision.HIGH
quad_scale = 1.0 / (4.0 * math.sqrt(2.0))


def shifted(block, axis, distance):
    devices = range(lax.axis_size(axis))
    route = [(i - distance, i) for i in devices if i - distance in devices]
    return lax.ppermute(block, axis, route)


def document_ids(lengths, positions):
    ends = jnp.cumsum(lengths, dtype=jnp.int32)
    counted = jnp.sum((ends[None, :] <= positions[:, None]).astype(jnp.int32), axis=1)
    return jnp.where(positions < 0, jnp.int32(-1), counted)


def pair_tables(width):
    rows, cols = np.triu_indices(width)
    quad_weight = np.where(rows == cols, quad_scale, quad_scale * math.sqrt(2.0))
    first = np.concatenate([[-1], np.full(width, -1), rows])
    second = np.concatenate([[-1], np.arange(width), cols])
    scale = np.concatenate([[1.0], np.full(width, 0.5), quad_weight]).astype(np.float32)
    feats = scale.size
    padded = -(-(feats + -(-feats // 128)) // 8) * 8
    extra = padded - feats
    first = np.concatenate([first, np.full(extra, width)])
    second = np.concatenate([second, np.full(extra, width)])
    scale = np.concatenate([scale, np.zeros(extra, np.float32)])
    dims = np.arange(width)
    pick_first = (first[:, None] == dims[None, :]).astype(np.float32)
    pick_second = (second[:, None] == dims[None, :]).astype(np.float32)
    return pick_first, (first < 0).astype(np.float32), pick_second, (second < 0).astype(np.float32), scale


def feature_rows(values):
    token_count, head_count, width = values.shape
    pick_first, one_first, pick_second, one_second, scale = pair_tables(width)
    picks = jnp.asarray(np.stack([pick_first, pick_second]), jnp.bfloat16)
    chosen = jnp.einsum("pfd,thd->phft", picks, values, preferred_element_type=jnp.float32)
    left = chosen[0] + jnp.asarray(one_first)[None, :, None]
    right = chosen[1] + jnp.asarray(one_second)[None, :, None]
    return (jnp.asarray(scale)[None, :, None] * left * right, (left, right))


def feature_grad(grad_phi, factors):
    left, right = factors
    width = 16
    pick_first, _, pick_second, _, scale = pair_tables(width)
    scaled = grad_phi * jnp.asarray(scale)[None, :, None]
    picks = jnp.asarray(np.concatenate([pick_first, pick_second], axis=0))
    both = jnp.concatenate([scaled * right, scaled * left], axis=1)
    return jnp.einsum("fd,hft->thd", picks, both, precision=high)


def block_flags(doc_lengths, devices, rows):
    firsts = jnp.arange(devices, dtype=jnp.int32) * rows
    prev_docs = document_ids(doc_lengths, firsts - 1)
    first_docs = document_ids(doc_lengths, firsts)
    last_docs = document_ids(doc_lengths, firsts + rows - 1)
    next_docs = document_ids(doc_lengths, firsts + rows)
    return (last_docs != prev_docs).astype(jnp.int32), (first_docs != next_docs).astype(jnp.int32)


def scan_masks(restart, closes):
    devices = restart.shape[0]
    order = jnp.arange(devices, dtype=jnp.int32)
    target = order[:, None]
    source = order[None, :]
    restarts_upto = jnp.cumsum(restart)
    closes_upto = jnp.cumsum(closes)
    gap_fwd = restarts_upto[jnp.maximum(target - 1, 0)] - restarts_upto[source]
    forward = (source < target) & (gap_fwd == 0)
    gap_bwd = closes_upto[jnp.maximum(source - 1, 0)] - closes_upto[target]
    backward = (source > target) & (gap_bwd == 0)
    return forward.astype(jnp.float32), backward.astype(jnp.float32)


def state_scan(local_state, local_norm, mask, filler):
    devices = mask.shape[0]
    heads, feats, width = local_state.shape
    norm_rows = -(-feats // width)
    room = feats - norm_rows
    norm_block = jnp.pad(local_norm, ((0, 0), (0, norm_rows * width - feats)))
    packed = lax.dynamic_update_slice(
        local_state, norm_block.reshape(heads, norm_rows, width), (0, room, 0)
    ).reshape(devices, -1, width)
    chunks = lax.all_to_all(packed, "ctx", 0, 0, tiled=True)
    chunks, filler = lax.optimization_barrier((chunks, filler))
    summed = jnp.einsum("ij,jrc->irc", mask, chunks, precision=high)
    back = lax.all_to_all(summed, "ctx", 0, 0, tiled=True).reshape(heads, feats, width)
    norm_in = back[:, room:].reshape(heads, norm_rows * width)[:, :feats]
    return (back, norm_in, filler)


def local(query, key, value_in, gate, conv_weight, doc_lengths, d_out):
    tok_rows = query.shape[0]
    channels = value_in.shape[1]
    dev_index = lax.axis_index("ctx")
    first_pos = dev_index * tok_rows
    local_pos = jnp.arange(tok_rows, dtype=jnp.int32)
    doc_ids = document_ids(doc_lengths, first_pos + local_pos)
    edge_docs = document_ids(doc_lengths, first_pos + jnp.array([-1, tok_rows], jnp.int32))
    prev_doc = edge_docs[0]
    next_doc = edge_docs[1]
    before_ids = document_ids(
        doc_lengths, first_pos - (CONV - 1) + jnp.arange(CONV - 1, dtype=jnp.int32)
    )
    after_ids = document_ids(
        doc_lengths, first_pos + tok_rows + jnp.arange(CONV - 1, dtype=jnp.int32)
    )
    taps = conv_weight.astype(jnp.float32)
    earlier = shifted(value_in[tok_rows - (CONV - 1) :], "ctx", 1)
    extended = jnp.concatenate([earlier, value_in], axis=0)
    extended_ids = jnp.concatenate([before_ids, doc_ids], axis=0)
    convolved = jnp.zeros((tok_rows, channels), jnp.float32)
    for offset in range(CONV):
        lower_row = CONV - 1 - offset
        keep = (extended_ids[lower_row : lower_row + tok_rows] == doc_ids).astype(jnp.float32)
        convolved = (
            convolved
            + taps[offset][None, :]
            * extended[lower_row : lower_row + tok_rows].astype(jnp.float32)
            * keep[:, None]
        )
    opening = jax.nn.sigmoid(gate.astype(jnp.float32))
    value_rows = (convolved * opening).astype(jnp.bfloat16)
    q_float = query.astype(jnp.float32).reshape(tok_rows, HEADS, KD)
    k_float = key.astype(jnp.float32).reshape(tok_rows, HEADS, KD)
    v_float = value_rows.astype(jnp.float32).reshape(tok_rows, HEADS, VD)
    scores = (
        jnp.einsum(
            "thd,shd->hts",
            query.reshape(tok_rows, HEADS, KD),
            key.reshape(tok_rows, HEADS, KD),
            preferred_element_type=jnp.float32,
        )
        * 0.25
    )
    kernel = 1.0 + scores + 0.5 * scores * scores
    allowed = (local_pos[:, None] >= local_pos[None, :]) & (doc_ids[:, None] == doc_ids[None, :])
    weights = jnp.where(allowed[None], kernel, 0.0)
    numerator = jnp.einsum("hts,shv->thv", weights, v_float, precision=high)
    denominator = jnp.transpose(jnp.sum(weights, axis=2), (1, 0))
    phi_query, spread_query = feature_rows(query.reshape(tok_rows, HEADS, KD))
    phi_key, spread_key = feature_rows(key.reshape(tok_rows, HEADS, KD))
    last_mask = (doc_ids == doc_ids[tok_rows - 1]).astype(jnp.float32)
    masked_key = phi_key * last_mask[None, None, :]
    local_state = jnp.einsum("hft,thv->hfv", masked_key, v_float, precision=high)
    local_norm = jnp.sum(masked_key, axis=2)
    restart_all, closes_all = block_flags(doc_lengths, lax.axis_size("ctx"), tok_rows)
    forward_mask, backward_mask = scan_masks(restart_all, closes_all)
    state_in, norm_in, denominator = state_scan(local_state, local_norm, forward_mask, denominator)
    inside = (doc_ids == prev_doc).astype(jnp.float32)
    numerator = numerator + inside[:, None, None] * jnp.einsum(
        "hft,hfv->thv", phi_query, state_in, precision=high
    )
    denominator = denominator + inside[:, None] * jnp.einsum(
        "hft,hf->th", phi_query, norm_in, precision=high
    )
    attended = numerator / denominator[:, :, None]
    mixed = attended.reshape(tok_rows, HEADS * VD).astype(jnp.bfloat16)
    upstream = d_out.astype(jnp.float32).reshape(tok_rows, HEADS, VD)
    grad_num = upstream / denominator[:, :, None]
    grad_den = -jnp.sum(upstream * attended, axis=2) / denominator
    first_mask = (doc_ids == doc_ids[0]).astype(jnp.float32)
    masked_query = phi_query * first_mask[None, None, :]
    back_state = jnp.einsum("hft,thv->hfv", masked_query, grad_num, precision=high)
    back_norm = jnp.einsum("hft,th->hf", masked_query, grad_den, precision=high)
    outside = (doc_ids == next_doc).astype(jnp.float32)
    grad_v = jnp.einsum("hts,thv->shv", weights, grad_num, precision=high)
    grad_weights = (
        jnp.einsum("thv,shv->hts", grad_num, v_float, precision=high)
        + jnp.transpose(grad_den, (1, 0))[:, :, None]
    )
    grad_scores = jnp.where(allowed[None], grad_weights * (1.0 + scores), 0.0)
    grad_q = jnp.einsum("hts,shd->thd", grad_scores, k_float, precision=high) * 0.25
    grad_k = jnp.einsum("hts,thd->shd", grad_scores, q_float, precision=high) * 0.25
    grad_phi_query = inside[None, None, :] * (
        jnp.einsum("hfv,thv->hft", state_in, grad_num, precision=high)
        + norm_in[:, :, None] * jnp.transpose(grad_den, (1, 0))[:, None, :]
    )
    grad_q = grad_q + feature_grad(grad_phi_query, spread_query)
    grad_state_in, grad_norm_in, (grad_v, grad_q, grad_k) = state_scan(
        back_state, back_norm, backward_mask, (grad_v, grad_q, grad_k)
    )
    grad_v = grad_v + outside[:, None, None] * jnp.einsum(
        "hfs,hfv->shv", phi_key, grad_state_in, precision=high
    )
    grad_phi_key = outside[None, None, :] * (
        jnp.einsum("hfv,shv->hfs", grad_state_in, v_float, precision=high)
        + grad_norm_in[:, :, None]
    )
    grad_k = grad_k + feature_grad(grad_phi_key, spread_key)
    grad_query = grad_q.reshape(tok_rows, HEADS * KD).astype(jnp.bfloat16)
    grad_key = grad_k.reshape(tok_rows, HEADS * KD).astype(jnp.bfloat16)
    grad_core = grad_v.reshape(tok_rows, channels)
    grad_gate = (grad_core * convolved * opening * (1.0 - opening)).astype(jnp.bfloat16)
    grad_conv = grad_core * opening
    later_rows = shifted(grad_conv[: CONV - 1], "ctx", -1)
    ahead = jnp.concatenate([grad_conv, later_rows], axis=0)
    ahead_ids = jnp.concatenate([doc_ids, after_ids], axis=0)
    grad_value = jnp.zeros((tok_rows, channels), jnp.float32)
    for offset in range(CONV):
        keep = (ahead_ids[offset : offset + tok_rows] == doc_ids).astype(jnp.float32)
        grad_value = (
            grad_value + taps[offset][None, :] * ahead[offset : offset + tok_rows] * keep[:, None]
        )
    return (mixed, grad_query, grad_key, grad_value.astype(jnp.bfloat16), grad_gate)


def solution(mesh):
    placed = (
        P(("dp", "ctx"), None),
        P(("dp", "ctx"), None),
        P(("dp", "ctx"), None),
        P(("dp", "ctx"), None),
        P(),
        P("dp"),
        P(("dp", "ctx"), None),
    )
    return jax.shard_map(
        local,
        mesh=mesh,
        in_specs=placed,
        out_specs=(
            P(("dp", "ctx"), None),
            P(("dp", "ctx"), None),
            P(("dp", "ctx"), None),
            P(("dp", "ctx"), None),
            P(("dp", "ctx"), None),
        ),
        check_vma=False,
    )
```
